32 devices in a mesh: wide: 8 (over z, x), narrow: 4 (over y, core).
Axes of the slice: x: 2, y: 2, z: 4, core: 2. Of those that a mesh axis runs over, the one named last changes fastest.
Arguments:
- sky_map: float32 [96, 192, 256], P('wide', 'narrow'), may hold values from -50 to 50
- noise_weight: float32 [96, 192, 256], P('wide', 'narrow'), may hold values from 0.4 to 1.6
- power_spectrum: float32 [96, 192, 256], P('wide', 'narrow'), may hold values from 0.1 to 6, as said below
Outputs:
- solution: float32 [96, 192, 256], P('wide', 'narrow')
- residual: float32 [96, 192, 256], P('wide', 'narrow')
The draws below stay inside these ranges and needn't reach their ends.
Inputs may be any that keep to these rules, and one draw needn't show every extreme that they name: power_spectrum[i, j, l] equals power_spectrum[(96 - i) % 96, j, l], power_spectrum[i, (192 - j) % 192, l] and power_spectrum[i, j, (256 - l) % 256].
All inputs are finite; a program needn't handle non-finite values.
Results may differ from the reference program's by a relative error of at most 0.00028.
Values sent between devices are 32-bit elements; how exact they have to be, the bound alone decides.
No kernel may reach another device: no remote copies, remote signals or barrier semaphores. Data moves between devices by JAX's collectives and lax.ppermute only.
A program may use at most 64 MiB of HBM per device.

```python
import math
import jax
import jax.numpy as jnp

NZ = 256
ITERS = 2
NX = 96
NY = 192


def folded_index(length):
    counter = jnp.arange(length)
    return jnp.minimum(counter, (length - counter) % length)


def draw_sky_map(key, part):
    base_key, channel_key = jax.random.split(jax.random.fold_in(key, 101))
    across = jnp.arange(NX, dtype=jnp.float32) / max(NX - 1, 1)
    down_axis = jnp.arange(NY, dtype=jnp.float32) / max(NY - 1, 1)
    ramp = jnp.sqrt(3.0) ** (across[:, None, None] + down_axis[None, :, None])
    channel_gain = 3.0 ** jax.random.uniform(channel_key, (NZ,), jnp.float32)
    values = jax.random.truncated_normal(base_key, -4.0, 4.0, (NX, NY, NZ), jnp.float32)
    return (values * ramp * channel_gain[None, None, :]).astype(jnp.float32)


def draw_power_spectrum(key, part):
    uniform_part = jax.random.uniform(jax.random.fold_in(key, 202), (NX, NY, NZ), jnp.float32)
    fold_x = folded_index(NX)
    fold_y = folded_index(NY)
    fold_z = folded_index(NZ)
    exponent = uniform_part
    table = 0.1 * 60.0 ** exponent
    table = table[fold_x][:, fold_y][:, :, fold_z]
    return table.astype(jnp.float32)


def shard_levels(own_key, shape, cuts, smallest, largest):
    def one(axis_at, blocks):
        draws = jax.random.uniform(jax.random.fold_in(jax.random.fold_in(own_key, 6), axis_at), (blocks,), jnp.float32, smallest / len(cuts), largest / len(cuts))
        return jnp.repeat(jnp.exp(draws), shape[axis_at] // blocks).reshape((-1,) + (1,) * (len(shape) - axis_at - 1))

    loudness = one(*cuts[0])
    for cut in cuts[1:]:
        loudness = loudness * one(*cut)
    return loudness


def setup_inputs(seed: int = 0) -> dict:
    key_list = jax.random.split(jax.random.key(seed), 4)
    return {
        "sky_map": draw_sky_map(jax.random.fold_in(key_list[3], 71), 0),
        "noise_weight": jnp.clip(jnp.exp(math.log(1.6) - 1.3862944 * jax.random.uniform(key_list[1], (NX, NY, NZ), jnp.float32) ** shard_levels(key_list[1], (NX, NY, NZ), ((0, 8), (1, 4)), -0.2, 0.2)), 0.4, 1.6),
        "power_spectrum": draw_power_spectrum(jax.random.fold_in(key_list[3], 71), 0),
    }


def reference(sky_map, noise_weight, power_spectrum):
    half_depth = NZ // 2 + 1
    spectrum_half = power_spectrum[:, :, :half_depth]

    def operate(vector):
        whitened = noise_weight * vector
        smoothed = jnp.fft.irfftn(spectrum_half * jnp.fft.rfftn(whitened), s=(NX, NY, NZ))
        return vector + noise_weight * smoothed

    right_side = noise_weight * sky_map
    solution = jnp.zeros_like(right_side)
    residual = right_side
    direction = right_side
    norm_now = jnp.sum(residual * residual)
    for iteration in range(ITERS):
        applied = operate(direction)
        step_size = norm_now / jnp.sum(direction * applied)
        solution = solution + step_size * direction
        residual = residual - step_size * applied
        norm_next = jnp.sum(residual * residual)
        direction = residual + (norm_next / norm_now) * direction
        norm_now = norm_next
    return solution, residual
```

```python
import math

import jax
import jax.numpy as jnp
from jax import lax
from jax.sharding import PartitionSpec as P

ITERS = 2

AXES = ("wide", "narrow")

highest = lax.Precision.HIGHEST


def cas_matrix(length):
    counter = lax.iota(jnp.int32, length)
    phase = counter[:, None] * counter[None, :] % length
    angle = phase.astype(jnp.float32) * (2.0 * math.pi / length)
    return jnp.cos(angle) + jnp.sin(angle)


def contract(spec, values, matrix):
    return jnp.einsum(spec, values, matrix, precision=highest, preferred_element_type=jnp.float32)


def exchange(blocks):
    return lax.all_to_all(blocks, AXES, 0, 0, tiled=True)


def global_sums(partials):
    count = lax.axis_size("wide") * lax.axis_size("narrow")
    spread = jnp.broadcast_to(partials[None], (count,) + partials.shape)
    return jnp.sum(exchange(spread), axis=0)


def local(sky_map, noise_weight, power_spectrum):
    local_x, local_y, depth = sky_map.shape
    n_wide = lax.axis_size("wide")
    n_narrow = lax.axis_size("narrow")
    count = n_wide * n_narrow
    chunk = depth // count
    full_x = local_x * n_wide
    full_y = local_y * n_narrow
    matrix_x = cas_matrix(full_x).reshape(n_wide, local_x, full_x)
    matrix_y = cas_matrix(full_y).reshape(n_narrow, local_y, full_y)
    matrix_z = cas_matrix(depth)
    inverse_cells = 1.0 / float(full_x * full_y * depth)

    def to_planes(blocks):
        return blocks.reshape(n_wide, n_narrow, chunk, local_x, local_y)

    def forward_sky(planes):
        along_x = contract("wnkab,wax->nkxb", planes, matrix_x)
        return contract("nkxb,nby->kxy", along_x, matrix_y)

    def inverse_sky(spectral):
        along_y = contract("kxy,nby->nkxb", spectral, matrix_y)
        along_x = contract("nkxb,wax->wnkab", along_y, matrix_x)
        return along_x.reshape(count, chunk, local_x, local_y)

    def channel_blocks(values):
        return contract("abz,zk->kab", values, matrix_z).reshape(count, chunk, local_x, local_y)

    def finish(blocks):
        return contract("kab,kz->abz", blocks.reshape(depth, local_x, local_y), matrix_z)

    def smoothed_spectral(blocks, weights):
        return inverse_sky(forward_sky(to_planes(blocks)) * weights)

    right_side = noise_weight * sky_map

    power_blocks = jnp.transpose(power_spectrum, (2, 0, 1)).reshape(count, chunk, local_x, local_y)
    first = exchange(jnp.concatenate([channel_blocks(noise_weight * right_side), power_blocks], axis=1))
    power_planes = to_planes(first[:, chunk:])
    weights = (
        jnp.transpose(power_planes, (2, 0, 3, 1, 4)).reshape(chunk, full_x, full_y) * inverse_cells
    )

    def apply_from(blocks, vector):
        back = exchange(smoothed_spectral(blocks, weights))
        return vector + noise_weight * finish(back)

    image_1 = apply_from(first[:, :chunk], right_side)
    image_2 = apply_from(exchange(channel_blocks(noise_weight * image_1)), image_1)
    moments = global_sums(
        jnp.stack(
            [
                jnp.sum(right_side * right_side),
                jnp.sum(right_side * image_1),
                jnp.sum(image_1 * image_1),
                jnp.sum(image_1 * image_2),
            ]
        )
    )
    norm_0, curvature_1, image_norm, cross = moments[0], moments[1], moments[2], moments[3]
    step_1 = norm_0 / curvature_1
    norm_1 = norm_0 - 2.0 * step_1 * curvature_1 + step_1 * step_1 * image_norm
    grow = 1.0 + norm_1 / norm_0
    curvature_2 = grow * grow * curvature_1 - 2.0 * step_1 * grow * image_norm + step_1 * step_1 * cross
    step_2 = norm_1 / curvature_2
    lead = step_1 + step_2 * grow
    tail = step_2 * step_1
    solution = lead * right_side - tail * image_1
    residual = right_side - lead * image_1 + tail * image_2
    return (solution, residual)


def solution(mesh):
    return jax.shard_map(
        local,
        mesh=mesh,
        in_specs=(P("wide", "narrow", None), P("wide", "narrow", None), P("wide", "narrow", None)),
        out_specs=(P("wide", "narrow", None), P("wide", "narrow", None)),
        check_vma=False,
    )
```

```python
import math

import jax
import jax.numpy as jnp
from jax import lax
from jax.sharding import PartitionSpec as P

ITERS = 2

AXES = ("wide", "narrow")

highest = lax.Precision.HIGHEST


def cas_matrix(length):
    counter = lax.iota(jnp.int32, length)
    phase = counter[:, None] * counter[None, :] % length
    angle = phase.astype(jnp.float32) * (2.0 * math.pi / length)
    return jnp.cos(angle) + jnp.sin(angle)


def contract(spec, values, matrix):
    return jnp.einsum(spec, values, matrix, precision=highest, preferred_element_type=jnp.float32)


def exchange(blocks):
    return lax.all_to_all(blocks, AXES, 0, 0, tiled=True)


def global_sums(partials):
    count = lax.axis_size("wide") * lax.axis_size("narrow")
    spread = jnp.broadcast_to(partials[None], (count,) + partials.shape)
    return jnp.sum(exchange(spread), axis=0)


def local(sky_map, noise_weight, power_spectrum):
    local_x, local_y, depth = sky_map.shape
    n_wide = lax.axis_size("wide")
    n_narrow = lax.axis_size("narrow")
    count = n_wide * n_narrow
    chunk = depth // count
    full_x = local_x * n_wide
    full_y = local_y * n_narrow
    matrix_x = cas_matrix(full_x).reshape(n_wide, local_x, full_x)
    matrix_y = cas_matrix(full_y).reshape(n_narrow, local_y, full_y)
    matrix_z = cas_matrix(depth)
    inverse_cells = 1.0 / float(full_x * full_y * depth)

    def to_planes(blocks):
        return blocks.reshape(n_wide, n_narrow, chunk, local_x, local_y)

    def forward_sky(planes):
        along_x = contract("wnkab,wax->nkxb", planes, matrix_x)
        return contract("nkxb,nby->kxy", along_x, matrix_y)

    def inverse_sky(spectral):
        along_y = contract("kxy,nby->nkxb", spectral, matrix_y)
        along_x = contract("nkxb,wax->wnkab", along_y, matrix_x)
        return along_x.reshape(count, chunk, local_x, local_y)

    def channel_blocks(values):
        return contract("abz,zk->kab", values, matrix_z).reshape(count, chunk, local_x, local_y)

    def finish(blocks):
        return contract("kab,kz->abz", blocks.reshape(depth, local_x, local_y), matrix_z)

    def smoothed_spectral(blocks, weights):
        return inverse_sky(forward_sky(to_planes(blocks)) * weights)

    right_side = noise_weight * sky_map

    power_blocks = jnp.transpose(power_spectrum, (2, 0, 1)).reshape(count, chunk, local_x, local_y)
    first = exchange(jnp.concatenate([channel_blocks(noise_weight * right_side), power_blocks], axis=1))
    power_planes = to_planes(first[:, chunk:])
    weights = (
        jnp.transpose(power_planes, (2, 0, 3, 1, 4)).reshape(chunk, full_x, full_y) * inverse_cells
    )

    def apply_from(blocks, vector):
        back = exchange(smoothed_spectral(blocks, weights))
        return vector + noise_weight * finish(back)

    image_1 = apply_from(first[:, :chunk], right_side)
    image_2 = apply_from(exchange(channel_blocks(noise_weight * image_1)), image_1)
    lanes = 128

    def lane_sums(left, right):
        return jnp.sum((left * right).reshape(-1, depth // lanes, lanes), axis=(0, 1))

    partials = jnp.stack(
        [
            lane_sums(right_side, right_side),
            lane_sums(right_side, image_1),
            lane_sums(image_1, image_1),
            lane_sums(image_1, image_2),
        ]
    )
    totals = contract("vl,lm->vm", global_sums(partials), jnp.ones((lanes, lanes), jnp.float32))
    moments = jnp.tile(totals, (1, depth // lanes)).reshape(4, 1, 1, depth)
    norm_0, curvature_1, image_norm, cross = moments[0], moments[1], moments[2], moments[3]
    step_1 = norm_0 / curvature_1
    norm_1 = norm_0 - 2.0 * step_1 * curvature_1 + step_1 * step_1 * image_norm
    grow = 1.0 + norm_1 / norm_0
    curvature_2 = grow * grow * curvature_1 - 2.0 * step_1 * grow * image_norm + step_1 * step_1 * cross
    step_2 = norm_1 / curvature_2
    lead = step_1 + step_2 * grow
    tail = step_2 * step_1
    solution = lead * right_side - tail * image_1
    residual = right_side - lead * image_1 + tail * image_2
    return (solution, residual)


def solution(mesh):
    return jax.shard_map(
        local,
        mesh=mesh,
        in_specs=(P("wide", "narrow", None), P("wide", "narrow", None), P("wide", "narrow", None)),
        out_specs=(P("wide", "narrow", None), P("wide", "narrow", None)),
        check_vma=False,
    )
```

```python
import math

import jax
import jax.numpy as jnp
from jax import lax
from jax.sharding import PartitionSpec as P

ITERS = 2

AXES = ("wide", "narrow")

highest = lax.Precision.HIGHEST


def cas_matrix(length, columns=None):
    counter = lax.iota(jnp.int32, length)
    frequency = counter if columns is None else jnp.asarray(columns, jnp.int32)
    phase = counter[:, None] * frequency[None, :] % length
    angle = phase.astype(jnp.float32) * (2.0 * math.pi / length)
    return jnp.cos(angle) + jnp.sin(angle)


def channel_plan(depth, count):
    chunk = depth // count
    if chunk % 2 or depth % 2:
        order = list(range(depth))
        return order, order, [list(range(chunk))] * count, chunk
    units = [[0], [depth // 2]] + [[k, depth - k] for k in range(1, depth // 2)]
    blocks, current = [], []
    for unit in units:
        current.append(unit)
        if sum(len(u) for u in current) == chunk:
            blocks.append(current)
            current = []
    reps = max(len(block) for block in blocks)
    order, chosen, slots = [], [], []
    for block in blocks:
        order += [c for unit in block for c in unit]
        firsts = [unit[0] for unit in block]
        chosen += firsts + [firsts[0]] * (reps - len(firsts))
        slots.append([i for i, unit in enumerate(block) for _ in unit])
    return order, chosen, slots, reps


def contract(spec, values, matrix):
    return jnp.einsum(spec, values, matrix, precision=highest, preferred_element_type=jnp.float32)


def exchange(blocks):
    return lax.all_to_all(blocks, AXES, 0, 0, tiled=True)


def global_sums(partials):
    count = lax.axis_size("wide") * lax.axis_size("narrow")
    spread = jnp.broadcast_to(partials[None], (count,) + partials.shape)
    return jnp.sum(exchange(spread), axis=0)


def local(sky_map, noise_weight, power_spectrum):
    local_x, local_y, depth = sky_map.shape
    n_wide = lax.axis_size("wide")
    n_narrow = lax.axis_size("narrow")
    count = n_wide * n_narrow
    chunk = depth // count
    full_x = local_x * n_wide
    full_y = local_y * n_narrow
    matrix_x = cas_matrix(full_x).reshape(n_wide, local_x, full_x)
    matrix_y = cas_matrix(full_y).reshape(n_narrow, local_y, full_y)
    order, chosen, slots, reps = channel_plan(depth, count)
    matrix_z = cas_matrix(depth, order)
    inverse_cells = 1.0 / float(full_x * full_y * depth)

    def to_planes_of(blocks, rows):
        return blocks.reshape(n_wide, n_narrow, rows, local_x, local_y)

    def to_planes(blocks):
        return to_planes_of(blocks, chunk)

    def forward_sky(planes):
        along_x = contract("wnkab,wax->nkxb", planes, matrix_x)
        return contract("nkxb,nby->kxy", along_x, matrix_y)

    def inverse_sky(spectral):
        along_y = contract("kxy,nby->nkxb", spectral, matrix_y)
        along_x = contract("nkxb,wax->wnkab", along_y, matrix_x)
        return along_x.reshape(count, chunk, local_x, local_y)

    def channel_blocks(values):
        return contract("abz,zk->kab", values, matrix_z).reshape(count, chunk, local_x, local_y)

    def finish(blocks):
        return contract("kab,zk->abz", blocks.reshape(depth, local_x, local_y), matrix_z)

    def smoothed_spectral(blocks, weights):
        return inverse_sky(forward_sky(to_planes(blocks)) * weights)

    right_side = noise_weight * sky_map

    power_blocks = jnp.transpose(
        jnp.take(power_spectrum, jnp.asarray(chosen, jnp.int32), axis=2), (2, 0, 1)
    ).reshape(count, reps, local_x, local_y)
    first = exchange(jnp.concatenate([channel_blocks(noise_weight * right_side), power_blocks], axis=1))
    power_planes = jnp.transpose(to_planes_of(first[:, chunk:], reps), (2, 0, 3, 1, 4)).reshape(
        reps, full_x, full_y
    )
    device = lax.axis_index("wide") * n_narrow + lax.axis_index("narrow")
    own_slots = jnp.asarray(slots, jnp.int32)[device]
    weights = jnp.take(power_planes, own_slots, axis=0) * inverse_cells

    def apply_from(blocks, vector):
        back = exchange(smoothed_spectral(blocks, weights))
        return vector + noise_weight * finish(back)

    image_1 = apply_from(first[:, :chunk], right_side)
    image_2 = apply_from(exchange(channel_blocks(noise_weight * image_1)), image_1)
    lanes = 128

    def lane_sums(left, right):
        return jnp.sum((left * right).reshape(-1, depth // lanes, lanes), axis=(0, 1))

    partials = jnp.stack(
        [
            lane_sums(right_side, right_side),
            lane_sums(right_side, image_1),
            lane_sums(image_1, image_1),
            lane_sums(image_1, image_2),
        ]
    )
    totals = contract("vl,lm->vm", global_sums(partials), jnp.ones((lanes, lanes), jnp.float32))
    moments = jnp.tile(totals, (1, depth // lanes)).reshape(4, 1, 1, depth)
    norm_0, curvature_1, image_norm, cross = moments[0], moments[1], moments[2], moments[3]
    step_1 = norm_0 / curvature_1
    norm_1 = norm_0 - 2.0 * step_1 * curvature_1 + step_1 * step_1 * image_norm
    grow = 1.0 + norm_1 / norm_0
    curvature_2 = grow * grow * curvature_1 - 2.0 * step_1 * grow * image_norm + step_1 * step_1 * cross
    step_2 = norm_1 / curvature_2
    lead = step_1 + step_2 * grow
    tail = step_2 * step_1
    solution = lead * right_side - tail * image_1
    residual = right_side - lead * image_1 + tail * image_2
    return (solution, residual)


def solution(mesh):
    return jax.shard_map(
        local,
        mesh=mesh,
        in_specs=(P("wide", "narrow", None), P("wide", "narrow", None), P("wide", "narrow", None)),
        out_specs=(P("wide", "narrow", None), P("wide", "narrow", None)),
        check_vma=False,
    )
```

```python
import math

import jax
import jax.numpy as jnp
from jax import lax
from jax.sharding import PartitionSpec as P

ITERS = 2

AXES = ("wide", "narrow")

highest = lax.Precision.HIGHEST


def cas_matrix(length, columns=None):
    counter = lax.iota(jnp.int32, length)
    frequency = counter if columns is None else jnp.asarray(columns, jnp.int32)
    phase = counter[:, None] * frequency[None, :] % length
    angle = phase.astype(jnp.float32) * (2.0 * math.pi / length)
    return jnp.cos(angle) + jnp.sin(angle)


def channel_order(depth, count):
    chunk = depth // count
    if chunk % 2:
        return list(range(depth)), False
    half = chunk // 2
    order = [0, depth // 2]
    for k in range(1, half):
        order += [k, depth - k]
    for k in range(half, depth // 2):
        order += [k, depth - k]
    return order, True


def contract(spec, values, matrix):
    return jnp.einsum(spec, values, matrix, precision=highest, preferred_element_type=jnp.float32)


def exchange(blocks):
    return lax.all_to_all(blocks, AXES, 0, 0, tiled=True)


def global_sums(partials):
    count = lax.axis_size("wide") * lax.axis_size("narrow")
    spread = jnp.broadcast_to(partials[None], (count,) + partials.shape)
    return jnp.sum(exchange(spread), axis=0)


def local(sky_map, noise_weight, power_spectrum):
    local_x, local_y, depth = sky_map.shape
    n_wide = lax.axis_size("wide")
    n_narrow = lax.axis_size("narrow")
    count = n_wide * n_narrow
    chunk = depth // count
    full_x = local_x * n_wide
    full_y = local_y * n_narrow
    matrix_x = cas_matrix(full_x).reshape(n_wide, local_x, full_x)
    matrix_y = cas_matrix(full_y).reshape(n_narrow, local_y, full_y)
    order, paired = channel_order(depth, count)
    matrix_z = cas_matrix(depth, order)
    inverse_cells = 1.0 / float(full_x * full_y * depth)

    def to_planes_of(blocks, rows):
        return blocks.reshape(n_wide, n_narrow, rows, local_x, local_y)

    def to_planes(blocks):
        return to_planes_of(blocks, chunk)

    def forward_sky(planes):
        along_x = contract("wnkab,wax->nkxb", planes, matrix_x)
        return contract("nkxb,nby->kxy", along_x, matrix_y)

    def inverse_sky(spectral):
        along_y = contract("kxy,nby->nkxb", spectral, matrix_y)
        along_x = contract("nkxb,wax->wnkab", along_y, matrix_x)
        return along_x.reshape(count, chunk, local_x, local_y)

    def channel_blocks(values):
        return contract("abz,zk->kab", values, matrix_z).reshape(count, chunk, local_x, local_y)

    def finish(blocks):
        return contract("kab,zk->abz", blocks.reshape(depth, local_x, local_y), matrix_z)

    def smoothed_spectral(blocks, weights):
        return inverse_sky(forward_sky(to_planes(blocks)) * weights)

    right_side = noise_weight * sky_map

    if paired:
        half = chunk // 2
        main = jnp.transpose(power_spectrum[:, :, : depth // 2], (2, 0, 1)).reshape(
            count, half, local_x, local_y
        )
        middle = jnp.broadcast_to(
            power_spectrum[None, None, :, :, depth // 2], (count, 1, local_x, local_y)
        )
        power_blocks = jnp.concatenate([main, middle], axis=1)
        rows = half + 1
    else:
        power_blocks = jnp.transpose(power_spectrum, (2, 0, 1)).reshape(count, chunk, local_x, local_y)
        rows = chunk
    first = exchange(jnp.concatenate([channel_blocks(noise_weight * right_side), power_blocks], axis=1))
    power_planes = jnp.transpose(to_planes_of(first[:, chunk:], rows), (2, 0, 3, 1, 4)).reshape(
        rows, full_x, full_y
    )
    if paired:
        device = lax.axis_index("wide") * n_narrow + lax.axis_index("narrow")
        second = jnp.where(device == 0, power_planes[half], power_planes[0])
        weights = jnp.concatenate(
            [power_planes[0:1], second[None], jnp.repeat(power_planes[1:half], 2, axis=0)], axis=0
        )
    else:
        weights = power_planes
    weights = weights * inverse_cells

    def apply_from(blocks, vector):
        back = exchange(smoothed_spectral(blocks, weights))
        return vector + noise_weight * finish(back)

    image_1 = apply_from(first[:, :chunk], right_side)
    image_2 = apply_from(exchange(channel_blocks(noise_weight * image_1)), image_1)
    lanes = 128

    def lane_sums(left, right):
        return jnp.sum((left * right).reshape(-1, depth // lanes, lanes), axis=(0, 1))

    partials = jnp.stack(
        [
            lane_sums(right_side, right_side),
            lane_sums(right_side, image_1),
            lane_sums(image_1, image_1),
            lane_sums(image_1, image_2),
        ]
    )
    totals = contract("vl,lm->vm", global_sums(partials), jnp.ones((lanes, lanes), jnp.float32))
    moments = jnp.tile(totals, (1, depth // lanes)).reshape(4, 1, 1, depth)
    norm_0, curvature_1, image_norm, cross = moments[0], moments[1], moments[2], moments[3]
    step_1 = norm_0 / curvature_1
    norm_1 = norm_0 - 2.0 * step_1 * curvature_1 + step_1 * step_1 * image_norm
    grow = 1.0 + norm_1 / norm_0
    curvature_2 = grow * grow * curvature_1 - 2.0 * step_1 * grow * image_norm + step_1 * step_1 * cross
    step_2 = norm_1 / curvature_2
    lead = step_1 + step_2 * grow
    tail = step_2 * step_1
    solution = lead * right_side - tail * image_1
    residual = right_side - lead * image_1 + tail * image_2
    return (solution, residual)


def solution(mesh):
    return jax.shard_map(
        local,
        mesh=mesh,
        in_specs=(P("wide", "narrow", None), P("wide", "narrow", None), P("wide", "narrow", None)),
        out_specs=(P("wide", "narrow", None), P("wide", "narrow", None)),
        check_vma=False,
    )
```

```python
import math

import jax
import jax.numpy as jnp
import numpy as np
from jax import lax
from jax.sharding import PartitionSpec as P

ITERS = 2

AXES = ("wide", "narrow")

highest = lax.Precision.HIGHEST


def cas_matrix(length, columns=None):
    counter = np.arange(length, dtype=np.int64)
    frequency = counter if columns is None else np.asarray(columns, np.int64)
    phase = counter[:, None] * frequency[None, :] % length
    angle = phase.astype(np.float64) * (2.0 * math.pi / length)
    return jnp.asarray((np.cos(angle) + np.sin(angle)).astype(np.float32))


def channel_order(depth, count):
    chunk = depth // count
    if chunk % 2:
        return list(range(depth)), False
    half = chunk // 2
    order = [0, depth // 2]
    for k in range(1, half):
        order += [k, depth - k]
    for k in range(half, depth // 2):
        order += [k, depth - k]
    return order, True


def contract(spec, values, matrix):
    return jnp.einsum(spec, values, matrix, precision=highest, preferred_element_type=jnp.float32)


def exchange(blocks):
    return lax.all_to_all(blocks, AXES, 0, 0, tiled=True)


def global_sums(partials):
    count = lax.axis_size("wide") * lax.axis_size("narrow")
    spread = jnp.broadcast_to(partials[None], (count,) + partials.shape)
    return jnp.sum(exchange(spread), axis=0)


def local(sky_map, noise_weight, power_spectrum):
    local_x, local_y, depth = sky_map.shape
    n_wide = lax.axis_size("wide")
    n_narrow = lax.axis_size("narrow")
    count = n_wide * n_narrow
    chunk = depth // count
    full_x = local_x * n_wide
    full_y = local_y * n_narrow
    matrix_x = cas_matrix(full_x).reshape(n_wide, local_x, full_x)
    matrix_y = cas_matrix(full_y).reshape(n_narrow, local_y, full_y)
    order, paired = channel_order(depth, count)
    matrix_z = cas_matrix(depth, order)
    inverse_cells = 1.0 / float(full_x * full_y * depth)

    def to_planes_of(blocks, rows):
        return blocks.reshape(n_wide, n_narrow, rows, local_x, local_y)

    def to_planes(blocks):
        return to_planes_of(blocks, chunk)

    def forward_sky(planes):
        along_x = contract("wnkab,wax->nkxb", planes, matrix_x)
        return contract("nkxb,nby->kxy", along_x, matrix_y)

    def inverse_sky(spectral):
        along_y = contract("kxy,nby->nkxb", spectral, matrix_y)
        along_x = contract("nkxb,wax->wnkab", along_y, matrix_x)
        return along_x.reshape(count, chunk, local_x, local_y)

    def channel_blocks(values):
        return contract("abz,zk->kab", values, matrix_z).reshape(count, chunk, local_x, local_y)

    def finish(blocks):
        return contract("kab,zk->abz", blocks.reshape(depth, local_x, local_y), matrix_z)

    def smoothed_spectral(blocks, weights):
        return inverse_sky(forward_sky(to_planes(blocks)) * weights)

    right_side = noise_weight * sky_map

    if paired:
        half = chunk // 2
        main = jnp.transpose(power_spectrum[:, :, : depth // 2], (2, 0, 1)).reshape(
            count, half, local_x, local_y
        )
        middle = jnp.broadcast_to(
            power_spectrum[None, None, :, :, depth // 2], (count, 1, local_x, local_y)
        )
        power_blocks = jnp.concatenate([main, middle], axis=1)
        rows = half + 1
    else:
        power_blocks = jnp.transpose(power_spectrum, (2, 0, 1)).reshape(count, chunk, local_x, local_y)
        rows = chunk
    first = exchange(jnp.concatenate([channel_blocks(noise_weight * right_side), power_blocks], axis=1))
    power_planes = jnp.transpose(to_planes_of(first[:, chunk:], rows), (2, 0, 3, 1, 4)).reshape(
        rows, full_x, full_y
    )
    if paired:
        device = lax.axis_index("wide") * n_narrow + lax.axis_index("narrow")
        second = jnp.where(device == 0, power_planes[half], power_planes[0])
        weights = jnp.concatenate(
            [power_planes[0:1], second[None], jnp.repeat(power_planes[1:half], 2, axis=0)], axis=0
        )
    else:
        weights = power_planes
    weights = weights * inverse_cells

    def apply_from(blocks, vector):
        back = exchange(smoothed_spectral(blocks, weights))
        return vector + noise_weight * finish(back)

    image_1 = apply_from(first[:, :chunk], right_side)
    image_2 = apply_from(exchange(channel_blocks(noise_weight * image_1)), image_1)
    lanes = 128

    def lane_sums(left, right):
        return jnp.sum((left * right).reshape(-1, depth // lanes, lanes), axis=(0, 1))

    partials = jnp.stack(
        [
            lane_sums(right_side, right_side),
            lane_sums(right_side, image_1),
            lane_sums(image_1, image_1),
            lane_sums(image_1, image_2),
        ]
    )
    totals = contract("vl,lm->vm", global_sums(partials), jnp.ones((lanes, lanes), jnp.float32))
    moments = jnp.tile(totals, (1, depth // lanes)).reshape(4, 1, 1, depth)
    norm_0, curvature_1, image_norm, cross = moments[0], moments[1], moments[2], moments[3]
    step_1 = norm_0 / curvature_1
    norm_1 = norm_0 - 2.0 * step_1 * curvature_1 + step_1 * step_1 * image_norm
    grow = 1.0 + norm_1 / norm_0
    curvature_2 = grow * grow * curvature_1 - 2.0 * step_1 * grow * image_norm + step_1 * step_1 * cross
    step_2 = norm_1 / curvature_2
    lead = step_1 + step_2 * grow
    tail = step_2 * step_1
    solution = lead * right_side - tail * image_1
    residual = right_side - lead * image_1 + tail * image_2
    return (solution, residual)


def solution(mesh):
    return jax.shard_map(
        local,
        mesh=mesh,
        in_specs=(P("wide", "narrow", None), P("wide", "narrow", None), P("wide", "narrow", None)),
        out_specs=(P("wide", "narrow", None), P("wide", "narrow", None)),
        check_vma=False,
    )
```

```python
import math

import jax
import jax.numpy as jnp
import numpy as np
from jax import lax
from jax.sharding import PartitionSpec as P

ITERS = 2

AXES = ("wide", "narrow")

highest = lax.Precision.HIGHEST


def cas_matrix(length, columns=None):
    counter = np.arange(length, dtype=np.int64)
    frequency = counter if columns is None else np.asarray(columns, np.int64)
    phase = counter[:, None] * frequency[None, :] % length
    angle = phase.astype(np.float64) * (2.0 * math.pi / length)
    return jnp.asarray((np.cos(angle) + np.sin(angle)).astype(np.float32))


def channel_order(depth, count):
    chunk = depth // count
    if chunk % 2:
        return list(range(depth)), False
    half = chunk // 2
    order = [0, depth // 2]
    for k in range(1, half):
        order += [k, depth - k]
    for k in range(half, depth // 2):
        order += [k, depth - k]
    return order, True


def contract(spec, values, matrix):
    return jnp.einsum(spec, values, matrix, precision=highest, preferred_element_type=jnp.float32)


def exchange(blocks):
    return lax.all_to_all(blocks, AXES, 0, 0, tiled=True)


def global_sums(partials):
    count = lax.axis_size("wide") * lax.axis_size("narrow")
    spread = jnp.broadcast_to(partials[None], (count,) + partials.shape)
    return jnp.sum(exchange(spread), axis=0)


def local(sky_map, noise_weight, power_spectrum):
    local_x, local_y, depth = sky_map.shape
    n_wide = lax.axis_size("wide")
    n_narrow = lax.axis_size("narrow")
    count = n_wide * n_narrow
    chunk = depth // count
    full_x = local_x * n_wide
    full_y = local_y * n_narrow
    matrix_x = cas_matrix(full_x)
    matrix_y = cas_matrix(full_y)
    order, paired = channel_order(depth, count)
    matrix_z = cas_matrix(depth, order)
    inverse_cells = 1.0 / float(full_x * full_y * depth)

    def to_planes_of(blocks, rows):
        return blocks.reshape(n_wide, n_narrow, rows, local_x, local_y)

    def to_planes(blocks):
        return to_planes_of(blocks, chunk)

    def forward_sky(planes):
        whole = jnp.transpose(planes, (0, 3, 1, 4, 2)).reshape(full_x, full_y, chunk)
        along_y = contract("xyk,yq->xqk", whole, matrix_y)
        return contract("xqk,xp->pqk", along_y, matrix_x)

    def inverse_sky(spectral):
        along_x = contract("pqk,xp->xqk", spectral, matrix_x)
        along_y = contract("xqk,yq->xyk", along_x, matrix_y)
        blocks = jnp.transpose(
            along_y.reshape(n_wide, local_x, n_narrow, local_y, chunk), (0, 2, 4, 1, 3)
        )
        return blocks.reshape(count, chunk, local_x, local_y)

    def channel_blocks(values):
        return contract("abz,zk->kab", values, matrix_z).reshape(count, chunk, local_x, local_y)

    def finish(blocks):
        return contract("kab,zk->abz", blocks.reshape(depth, local_x, local_y), matrix_z)

    def smoothed_spectral(blocks, weights):
        return inverse_sky(forward_sky(to_planes(blocks)) * weights)

    right_side = noise_weight * sky_map

    if paired:
        half = chunk // 2
        main = jnp.transpose(power_spectrum[:, :, : depth // 2], (2, 0, 1)).reshape(
            count, half, local_x, local_y
        )
        middle = jnp.broadcast_to(
            power_spectrum[None, None, :, :, depth // 2], (count, 1, local_x, local_y)
        )
        power_blocks = jnp.concatenate([main, middle], axis=1)
        rows = half + 1
    else:
        power_blocks = jnp.transpose(power_spectrum, (2, 0, 1)).reshape(count, chunk, local_x, local_y)
        rows = chunk
    first = exchange(jnp.concatenate([channel_blocks(noise_weight * right_side), power_blocks], axis=1))
    power_planes = jnp.transpose(to_planes_of(first[:, chunk:], rows), (2, 0, 3, 1, 4)).reshape(
        rows, full_x, full_y
    )
    if paired:
        device = lax.axis_index("wide") * n_narrow + lax.axis_index("narrow")
        second = jnp.where(device == 0, power_planes[half], power_planes[0])
        weights = jnp.concatenate(
            [power_planes[0:1], second[None], jnp.repeat(power_planes[1:half], 2, axis=0)], axis=0
        )
    else:
        weights = power_planes
    weights = jnp.transpose(weights, (1, 2, 0)) * inverse_cells

    def apply_from(blocks, vector):
        back = exchange(smoothed_spectral(blocks, weights))
        return vector + noise_weight * finish(back)

    image_1 = apply_from(first[:, :chunk], right_side)
    image_2 = apply_from(exchange(channel_blocks(noise_weight * image_1)), image_1)
    lanes = 128

    def lane_sums(left, right):
        return jnp.sum((left * right).reshape(-1, depth // lanes, lanes), axis=(0, 1))

    partials = jnp.stack(
        [
            lane_sums(right_side, right_side),
            lane_sums(right_side, image_1),
            lane_sums(image_1, image_1),
            lane_sums(image_1, image_2),
        ]
    )
    totals = contract("vl,lm->vm", global_sums(partials), jnp.ones((lanes, lanes), jnp.float32))
    moments = jnp.tile(totals, (1, depth // lanes)).reshape(4, 1, 1, depth)
    norm_0, curvature_1, image_norm, cross = moments[0], moments[1], moments[2], moments[3]
    step_1 = norm_0 / curvature_1
    norm_1 = norm_0 - 2.0 * step_1 * curvature_1 + step_1 * step_1 * image_norm
    grow = 1.0 + norm_1 / norm_0
    curvature_2 = grow * grow * curvature_1 - 2.0 * step_1 * grow * image_norm + step_1 * step_1 * cross
    step_2 = norm_1 / curvature_2
    lead = step_1 + step_2 * grow
    tail = step_2 * step_1
    solution = lead * right_side - tail * image_1
    residual = right_side - lead * image_1 + tail * image_2
    return (solution, residual)


def solution(mesh):
    return jax.shard_map(
        local,
        mesh=mesh,
        in_specs=(P("wide", "narrow", None), P("wide", "narrow", None), P("wide", "narrow", None)),
        out_specs=(P("wide", "narrow", None), P("wide", "narrow", None)),
        check_vma=False,
    )
```

```python
import math

import jax
import jax.numpy as jnp
import numpy as np
from jax import lax
from jax.sharding import PartitionSpec as P

ITERS = 2

AXES = ("wide", "narrow")

highest = lax.Precision.HIGHEST


def cas_matrix(length, columns=None):
    counter = np.arange(length, dtype=np.int64)
    frequency = counter if columns is None else np.asarray(columns, np.int64)
    phase = counter[:, None] * frequency[None, :] % length
    angle = phase.astype(np.float64) * (2.0 * math.pi / length)
    return jnp.asarray((np.cos(angle) + np.sin(angle)).astype(np.float32))


def channel_order(depth, count):
    chunk = depth // count
    if chunk % 2:
        return list(range(depth)), False
    half = chunk // 2
    order = [0, depth // 2]
    for k in range(1, half):
        order += [k, depth - k]
    for k in range(half, depth // 2):
        order += [k, depth - k]
    return order, True


def contract(spec, values, matrix):
    return jnp.einsum(spec, values, matrix, precision=highest, preferred_element_type=jnp.float32)


def exchange(blocks):
    return lax.all_to_all(blocks, AXES, 0, 0, tiled=True)


def global_sums(partials):
    count = lax.axis_size("wide") * lax.axis_size("narrow")
    spread = jnp.broadcast_to(partials[None], (count,) + partials.shape)
    return jnp.sum(exchange(spread), axis=0)


def local(sky_map, noise_weight, power_spectrum):
    local_x, local_y, depth = sky_map.shape
    n_wide = lax.axis_size("wide")
    n_narrow = lax.axis_size("narrow")
    count = n_wide * n_narrow
    chunk = depth // count
    full_x = local_x * n_wide
    full_y = local_y * n_narrow
    matrix_x = cas_matrix(full_x).reshape(n_wide, local_x, full_x)
    matrix_y = cas_matrix(full_y).reshape(n_narrow, local_y, full_y)
    order, paired = channel_order(depth, count)
    matrix_z = cas_matrix(depth, order)
    inverse_cells = 1.0 / float(full_x * full_y * depth)

    def to_planes_of(blocks, rows):
        return blocks.reshape(n_wide, n_narrow, rows, local_x, local_y)

    def to_planes(blocks):
        return to_planes_of(blocks, chunk)

    def forward_sky(planes):
        along_x = contract("wnkab,wax->nkxb", planes, matrix_x)
        return contract("nkxb,nby->kxy", along_x, matrix_y)

    def inverse_sky(spectral):
        along_y = contract("kxy,nby->nkxb", spectral, matrix_y)
        along_x = contract("nkxb,wax->wnkab", along_y, matrix_x)
        return along_x.reshape(count, chunk, local_x, local_y)

    def channel_blocks(values):
        return contract("abz,zk->kab", values, matrix_z).reshape(count, chunk, local_x, local_y)

    def finish(blocks):
        return contract("kab,zk->abz", blocks.reshape(depth, local_x, local_y), matrix_z)

    def smoothed_spectral(blocks, weights):
        return inverse_sky(forward_sky(to_planes(blocks)) * weights)

    right_side = noise_weight * sky_map

    if paired:
        half = chunk // 2
        main = jnp.transpose(power_spectrum[:, :, : depth // 2], (2, 0, 1)).reshape(
            count, half, local_x, local_y
        )
        middle = jnp.broadcast_to(
            power_spectrum[None, None, :, :, depth // 2], (count, 1, local_x, local_y)
        )
        power_blocks = jnp.concatenate([main, middle], axis=1)
        rows = half + 1
    else:
        power_blocks = jnp.transpose(power_spectrum, (2, 0, 1)).reshape(count, chunk, local_x, local_y)
        rows = chunk
    first = exchange(jnp.concatenate([channel_blocks(noise_weight * right_side), power_blocks], axis=1))
    power_planes = jnp.transpose(to_planes_of(first[:, chunk:], rows), (2, 0, 3, 1, 4)).reshape(
        rows, full_x, full_y
    )
    if paired:
        device = lax.axis_index("wide") * n_narrow + lax.axis_index("narrow")
        second = jnp.where(device == 0, power_planes[half], power_planes[0])
        weights = jnp.concatenate(
            [power_planes[0:1], second[None], jnp.repeat(power_planes[1:half], 2, axis=0)], axis=0
        )
    else:
        weights = power_planes
    weights = weights * inverse_cells

    lanes = 128

    def lane_sums(left, right):
        return jnp.sum((left * right).reshape(-1, depth // lanes, lanes), axis=(0, 1))

    image_1 = right_side + noise_weight * finish(exchange(smoothed_spectral(first[:, :chunk], weights)))
    sent = exchange(channel_blocks(noise_weight * image_1))
    returned = smoothed_spectral(sent, weights)
    cross = jnp.sum(sent * returned, axis=(0, 1, 2))
    cross = jnp.pad(cross, (0, lanes - cross.shape[0] % lanes if cross.shape[0] % lanes else 0))
    cross = jnp.sum(cross.reshape(-1, lanes), axis=0)
    image_norm = lane_sums(image_1, image_1)
    partials = jnp.stack(
        [lane_sums(right_side, right_side), lane_sums(right_side, image_1), image_norm, image_norm + cross]
    )
    block = chunk * local_x * local_y
    back = exchange(
        jnp.concatenate(
            [jnp.broadcast_to(partials.reshape(1, 4 * lanes), (count, 4 * lanes)), returned.reshape(count, block)],
            axis=1,
        )
    )
    image_2 = image_1 + noise_weight * finish(back[:, 4 * lanes :].reshape(count, chunk, local_x, local_y))
    summed = jnp.sum(back[:, : 4 * lanes].reshape(count, 4, lanes), axis=0)
    totals = contract("vl,lm->vm", summed, jnp.ones((lanes, lanes), jnp.float32))
    moments = jnp.tile(totals, (1, depth // lanes)).reshape(4, 1, 1, depth)
    norm_0, curvature_1, image_norm, cross = moments[0], moments[1], moments[2], moments[3]
    step_1 = norm_0 / curvature_1
    norm_1 = norm_0 - 2.0 * step_1 * curvature_1 + step_1 * step_1 * image_norm
    grow = 1.0 + norm_1 / norm_0
    curvature_2 = grow * grow * curvature_1 - 2.0 * step_1 * grow * image_norm + step_1 * step_1 * cross
    step_2 = norm_1 / curvature_2
    lead = step_1 + step_2 * grow
    tail = step_2 * step_1
    solution = lead * right_side - tail * image_1
    residual = right_side - lead * image_1 + tail * image_2
    return (solution, residual)


def solution(mesh):
    return jax.shard_map(
        local,
        mesh=mesh,
        in_specs=(P("wide", "narrow", None), P("wide", "narrow", None), P("wide", "narrow", None)),
        out_specs=(P("wide", "narrow", None), P("wide", "narrow", None)),
        check_vma=False,
    )
```

```python
import math

import jax
import jax.numpy as jnp
import numpy as np
from jax import lax
from jax.sharding import PartitionSpec as P

ITERS = 2

AXES = ("wide", "narrow")

highest = lax.Precision.HIGHEST


def cas_matrix(length, columns=None):
    counter = np.arange(length, dtype=np.int64)
    frequency = counter if columns is None else np.asarray(columns, np.int64)
    phase = counter[:, None] * frequency[None, :] % length
    angle = phase.astype(np.float64) * (2.0 * math.pi / length)
    return jnp.asarray((np.cos(angle) + np.sin(angle)).astype(np.float32))


def channel_order(depth, count):
    chunk = depth // count
    if chunk % 2:
        return list(range(depth)), False
    half = chunk // 2
    order = [0, depth // 2]
    for k in range(1, half):
        order += [k, depth - k]
    for k in range(half, depth // 2):
        order += [k, depth - k]
    return order, True


def contract(spec, values, matrix):
    return jnp.einsum(spec, values, matrix, precision=highest, preferred_element_type=jnp.float32)


def exchange(blocks):
    return lax.all_to_all(blocks, AXES, 0, 0, tiled=True)


def global_sums(partials):
    count = lax.axis_size("wide") * lax.axis_size("narrow")
    spread = jnp.broadcast_to(partials[None], (count,) + partials.shape)
    return jnp.sum(exchange(spread), axis=0)


def local(sky_map, noise_weight, power_spectrum):
    local_x, local_y, depth = sky_map.shape
    n_wide = lax.axis_size("wide")
    n_narrow = lax.axis_size("narrow")
    count = n_wide * n_narrow
    chunk = depth // count
    full_x = local_x * n_wide
    full_y = local_y * n_narrow
    matrix_x = cas_matrix(full_x).reshape(n_wide, local_x, full_x)
    matrix_y = cas_matrix(full_y).reshape(n_narrow, local_y, full_y)
    order, paired = channel_order(depth, count)
    matrix_z = cas_matrix(depth, order)
    inverse_cells = 1.0 / float(full_x * full_y * depth)

    def to_planes_of(blocks, rows):
        return blocks.reshape(n_wide, n_narrow, rows, local_x, local_y)

    def to_planes(blocks):
        return to_planes_of(blocks, chunk)

    def forward_sky(planes):
        along_x = contract("wnkab,wax->nkxb", planes, matrix_x)
        return contract("nkxb,nby->kxy", along_x, matrix_y)

    def inverse_sky(spectral):
        along_y = contract("kxy,nby->nkxb", spectral, matrix_y)
        along_x = contract("nkxb,wax->wnkab", along_y, matrix_x)
        return along_x.reshape(count, chunk, local_x, local_y)

    def channel_blocks(values):
        return contract("abz,zk->kab", values, matrix_z).reshape(count, chunk, local_x, local_y)

    def finish(blocks):
        return contract("kab,zk->abz", blocks.reshape(depth, local_x, local_y), matrix_z)

    def smoothed_spectral(blocks, weights):
        return inverse_sky(forward_sky(to_planes(blocks)) * weights)

    right_side = noise_weight * sky_map

    if paired:
        half = chunk // 2
        main = jnp.transpose(power_spectrum[:, :, : depth // 2], (2, 0, 1)).reshape(
            count, half, local_x, local_y
        )
        middle = jnp.broadcast_to(
            power_spectrum[None, None, :, :, depth // 2], (count, 1, local_x, local_y)
        )
        power_blocks = jnp.concatenate([main, middle], axis=1)
        rows = half + 1
    else:
        power_blocks = jnp.transpose(power_spectrum, (2, 0, 1)).reshape(count, chunk, local_x, local_y)
        rows = chunk
    power_received = exchange(power_blocks)
    first = exchange(channel_blocks(noise_weight * right_side))
    power_planes = jnp.transpose(to_planes_of(power_received, rows), (2, 0, 3, 1, 4)).reshape(
        rows, full_x, full_y
    )
    if paired:
        device = lax.axis_index("wide") * n_narrow + lax.axis_index("narrow")
        second = jnp.where(device == 0, power_planes[half], power_planes[0])
        weights = jnp.concatenate(
            [power_planes[0:1], second[None], jnp.repeat(power_planes[1:half], 2, axis=0)], axis=0
        )
    else:
        weights = power_planes
    weights = weights * inverse_cells

    lanes = 128

    def lane_sums(left, right):
        return jnp.sum((left * right).reshape(-1, depth // lanes, lanes), axis=(0, 1))

    image_1 = right_side + noise_weight * finish(exchange(smoothed_spectral(first, weights)))
    sent = exchange(channel_blocks(noise_weight * image_1))
    returned = smoothed_spectral(sent, weights)
    cross = jnp.sum(sent * returned, axis=(0, 1, 2))
    cross = jnp.pad(cross, (0, lanes - cross.shape[0] % lanes if cross.shape[0] % lanes else 0))
    cross = jnp.sum(cross.reshape(-1, lanes), axis=0)
    image_norm = lane_sums(image_1, image_1)
    partials = jnp.stack(
        [lane_sums(right_side, right_side), lane_sums(right_side, image_1), image_norm, image_norm + cross]
    )
    block = chunk * local_x * local_y
    back = exchange(
        jnp.concatenate(
            [jnp.broadcast_to(partials.reshape(1, 4 * lanes), (count, 4 * lanes)), returned.reshape(count, block)],
            axis=1,
        )
    )
    image_2 = image_1 + noise_weight * finish(back[:, 4 * lanes :].reshape(count, chunk, local_x, local_y))
    summed = jnp.sum(back[:, : 4 * lanes].reshape(count, 4, lanes), axis=0)
    totals = contract("vl,lm->vm", summed, jnp.ones((lanes, lanes), jnp.float32))
    moments = jnp.tile(totals, (1, depth // lanes)).reshape(4, 1, 1, depth)
    norm_0, curvature_1, image_norm, cross = moments[0], moments[1], moments[2], moments[3]
    step_1 = norm_0 / curvature_1
    norm_1 = norm_0 - 2.0 * step_1 * curvature_1 + step_1 * step_1 * image_norm
    grow = 1.0 + norm_1 / norm_0
    curvature_2 = grow * grow * curvature_1 - 2.0 * step_1 * grow * image_norm + step_1 * step_1 * cross
    step_2 = norm_1 / curvature_2
    lead = step_1 + step_2 * grow
    tail = step_2 * step_1
    solution = lead * right_side - tail * image_1
    residual = right_side - lead * image_1 + tail * image_2
    return (solution, residual)


def solution(mesh):
    return jax.shard_map(
        local,
        mesh=mesh,
        in_specs=(P("wide", "narrow", None), P("wide", "narrow", None), P("wide", "narrow", None)),
        out_specs=(P("wide", "narrow", None), P("wide", "narrow", None)),
        check_vma=False,
    )
```

```python
import math

import jax
import jax.numpy as jnp
import numpy as np
from jax import lax
from jax.sharding import PartitionSpec as P

ITERS = 2

AXES = ("wide", "narrow")

highest = lax.Precision.HIGHEST


def cas_matrix(length, columns=None):
    counter = np.arange(length, dtype=np.int64)
    frequency = counter if columns is None else np.asarray(columns, np.int64)
    phase = counter[:, None] * frequency[None, :] % length
    angle = phase.astype(np.float64) * (2.0 * math.pi / length)
    return jnp.asarray((np.cos(angle) + np.sin(angle)).astype(np.float32))


def channel_order(depth, count):
    chunk = depth // count
    if chunk % 2:
        return list(range(depth)), False
    half = chunk // 2
    order = [0, depth // 2]
    for k in range(1, half):
        order += [k, depth - k]
    for k in range(half, depth // 2):
        order += [k, depth - k]
    return order, True


def contract(spec, values, matrix):
    return jnp.einsum(spec, values, matrix, precision=highest, preferred_element_type=jnp.float32)


def exchange(blocks):
    return lax.all_to_all(blocks, AXES, 0, 0, tiled=True)


def global_sums(partials):
    count = lax.axis_size("wide") * lax.axis_size("narrow")
    spread = jnp.broadcast_to(partials[None], (count,) + partials.shape)
    return jnp.sum(exchange(spread), axis=0)


def local(sky_map, noise_weight, power_spectrum):
    local_x, local_y, depth = sky_map.shape
    n_wide = lax.axis_size("wide")
    n_narrow = lax.axis_size("narrow")
    count = n_wide * n_narrow
    chunk = depth // count
    full_x = local_x * n_wide
    full_y = local_y * n_narrow
    matrix_x = cas_matrix(full_x).reshape(n_wide, local_x, full_x)
    matrix_y = cas_matrix(full_y).reshape(n_narrow, local_y, full_y)
    order, paired = channel_order(depth, count)
    matrix_z = cas_matrix(depth, order)
    inverse_cells = 1.0 / float(full_x * full_y * depth)

    def to_planes_of(blocks, rows):
        return blocks.reshape(n_wide, n_narrow, rows, local_x, local_y)

    def to_planes(blocks):
        return to_planes_of(blocks, chunk)

    def forward_sky(planes):
        along_y = contract("wnkab,nby->wkay", planes, matrix_y)
        return contract("wkay,wax->kxy", along_y, matrix_x)

    def inverse_sky(spectral):
        along_x = contract("kxy,wax->wkay", spectral, matrix_x)
        along_y = contract("wkay,nby->wnkab", along_x, matrix_y)
        return along_y.reshape(count, chunk, local_x, local_y)

    def channel_blocks(values):
        return contract("abz,zk->kab", values, matrix_z).reshape(count, chunk, local_x, local_y)

    def finish(blocks):
        return contract("kab,zk->abz", blocks.reshape(depth, local_x, local_y), matrix_z)

    def smoothed_spectral(blocks, weights):
        return inverse_sky(forward_sky(to_planes(blocks)) * weights)

    right_side = noise_weight * sky_map

    if paired:
        half = chunk // 2
        main = jnp.transpose(power_spectrum[:, :, : depth // 2], (2, 0, 1)).reshape(
            count, half, local_x, local_y
        )
        middle = jnp.broadcast_to(
            power_spectrum[None, None, :, :, depth // 2], (count, 1, local_x, local_y)
        )
        power_blocks = jnp.concatenate([main, middle], axis=1)
        rows = half + 1
    else:
        power_blocks = jnp.transpose(power_spectrum, (2, 0, 1)).reshape(count, chunk, local_x, local_y)
        rows = chunk
    power_received = exchange(power_blocks)
    first = exchange(channel_blocks(noise_weight * right_side))
    power_planes = jnp.transpose(to_planes_of(power_received, rows), (2, 0, 3, 1, 4)).reshape(
        rows, full_x, full_y
    )
    if paired:
        device = lax.axis_index("wide") * n_narrow + lax.axis_index("narrow")
        second = jnp.where(device == 0, power_planes[half], power_planes[0])
        weights = jnp.concatenate(
            [power_planes[0:1], second[None], jnp.repeat(power_planes[1:half], 2, axis=0)], axis=0
        )
    else:
        weights = power_planes
    weights = weights * inverse_cells

    lanes = 128

    def lane_sums(left, right):
        return jnp.sum((left * right).reshape(-1, depth // lanes, lanes), axis=(0, 1))

    image_1 = right_side + noise_weight * finish(exchange(smoothed_spectral(first, weights)))
    sent = exchange(channel_blocks(noise_weight * image_1))
    returned = smoothed_spectral(sent, weights)
    cross = jnp.sum(sent * returned, axis=(0, 1, 2))
    cross = jnp.pad(cross, (0, lanes - cross.shape[0] % lanes if cross.shape[0] % lanes else 0))
    cross = jnp.sum(cross.reshape(-1, lanes), axis=0)
    image_norm = lane_sums(image_1, image_1)
    partials = jnp.stack(
        [lane_sums(right_side, right_side), lane_sums(right_side, image_1), image_norm, image_norm + cross]
    )
    block = chunk * local_x * local_y
    back = exchange(
        jnp.concatenate(
            [jnp.broadcast_to(partials.reshape(1, 4 * lanes), (count, 4 * lanes)), returned.reshape(count, block)],
            axis=1,
        )
    )
    image_2 = image_1 + noise_weight * finish(back[:, 4 * lanes :].reshape(count, chunk, local_x, local_y))
    summed = jnp.sum(back[:, : 4 * lanes].reshape(count, 4, lanes), axis=0)
    totals = contract("vl,lm->vm", summed, jnp.ones((lanes, lanes), jnp.float32))
    moments = jnp.tile(totals, (1, depth // lanes)).reshape(4, 1, 1, depth)
    norm_0, curvature_1, image_norm, cross = moments[0], moments[1], moments[2], moments[3]
    step_1 = norm_0 / curvature_1
    norm_1 = norm_0 - 2.0 * step_1 * curvature_1 + step_1 * step_1 * image_norm
    grow = 1.0 + norm_1 / norm_0
    curvature_2 = grow * grow * curvature_1 - 2.0 * step_1 * grow * image_norm + step_1 * step_1 * cross
    step_2 = norm_1 / curvature_2
    lead = step_1 + step_2 * grow
    tail = step_2 * step_1
    solution = lead * right_side - tail * image_1
    residual = right_side - lead * image_1 + tail * image_2
    return (solution, residual)


def solution(mesh):
    return jax.shard_map(
        local,
        mesh=mesh,
        in_specs=(P("wide", "narrow", None), P("wide", "narrow", None), P("wide", "narrow", None)),
        out_specs=(P("wide", "narrow", None), P("wide", "narrow", None)),
        check_vma=False,
    )
```

```python
import math

import jax
import jax.numpy as jnp
import numpy as np
from jax import lax
from jax.sharding import PartitionSpec as P

ITERS = 2

AXES = ("wide", "narrow")

highest = lax.Precision.HIGHEST
transform = lax.Precision.HIGH


def cas_matrix(length, columns=None):
    counter = np.arange(length, dtype=np.int64)
    frequency = counter if columns is None else np.asarray(columns, np.int64)
    phase = counter[:, None] * frequency[None, :] % length
    angle = phase.astype(np.float64) * (2.0 * math.pi / length)
    return jnp.asarray((np.cos(angle) + np.sin(angle)).astype(np.float32))


def channel_order(depth, count):
    chunk = depth // count
    if chunk % 2:
        return list(range(depth)), False
    half = chunk // 2
    order = [0, depth // 2]
    for k in range(1, half):
        order += [k, depth - k]
    for k in range(half, depth // 2):
        order += [k, depth - k]
    return order, True


def contract(spec, values, matrix, precision=transform):
    return jnp.einsum(spec, values, matrix, precision=precision, preferred_element_type=jnp.float32)


def exchange(blocks):
    return lax.all_to_all(blocks, AXES, 0, 0, tiled=True)


def global_sums(partials):
    count = lax.axis_size("wide") * lax.axis_size("narrow")
    spread = jnp.broadcast_to(partials[None], (count,) + partials.shape)
    return jnp.sum(exchange(spread), axis=0)


def local(sky_map, noise_weight, power_spectrum):
    local_x, local_y, depth = sky_map.shape
    n_wide = lax.axis_size("wide")
    n_narrow = lax.axis_size("narrow")
    count = n_wide * n_narrow
    chunk = depth // count
    full_x = local_x * n_wide
    full_y = local_y * n_narrow
    matrix_x = cas_matrix(full_x).reshape(n_wide, local_x, full_x)
    matrix_y = cas_matrix(full_y).reshape(n_narrow, local_y, full_y)
    order, paired = channel_order(depth, count)
    matrix_z = cas_matrix(depth, order)
    inverse_cells = 1.0 / float(full_x * full_y * depth)

    def to_planes_of(blocks, rows):
        return blocks.reshape(n_wide, n_narrow, rows, local_x, local_y)

    def to_planes(blocks):
        return to_planes_of(blocks, chunk)

    def forward_sky(planes):
        along_y = contract("wnkab,nby->wkay", planes, matrix_y)
        return contract("wkay,wax->kxy", along_y, matrix_x)

    def inverse_sky(spectral):
        along_x = contract("kxy,wax->wkay", spectral, matrix_x)
        along_y = contract("wkay,nby->wnkab", along_x, matrix_y)
        return along_y.reshape(count, chunk, local_x, local_y)

    def channel_blocks(values):
        return contract("abz,zk->kab", values, matrix_z).reshape(count, chunk, local_x, local_y)

    def finish(blocks):
        return contract("kab,zk->abz", blocks.reshape(depth, local_x, local_y), matrix_z)

    def smoothed_spectral(blocks, weights):
        return inverse_sky(forward_sky(to_planes(blocks)) * weights)

    right_side = noise_weight * sky_map

    if paired:
        half = chunk // 2
        main = jnp.transpose(power_spectrum[:, :, : depth // 2], (2, 0, 1)).reshape(
            count, half, local_x, local_y
        )
        middle = jnp.broadcast_to(
            power_spectrum[None, None, :, :, depth // 2], (count, 1, local_x, local_y)
        )
        power_blocks = jnp.concatenate([main, middle], axis=1)
        rows = half + 1
    else:
        power_blocks = jnp.transpose(power_spectrum, (2, 0, 1)).reshape(count, chunk, local_x, local_y)
        rows = chunk
    power_received = exchange(power_blocks)
    first = exchange(channel_blocks(noise_weight * right_side))
    power_planes = jnp.transpose(to_planes_of(power_received, rows), (2, 0, 3, 1, 4)).reshape(
        rows, full_x, full_y
    )
    if paired:
        device = lax.axis_index("wide") * n_narrow + lax.axis_index("narrow")
        second = jnp.where(device == 0, power_planes[half], power_planes[0])
        weights = jnp.concatenate(
            [power_planes[0:1], second[None], jnp.repeat(power_planes[1:half], 2, axis=0)], axis=0
        )
    else:
        weights = power_planes
    weights = weights * inverse_cells

    lanes = 128

    def lane_sums(left, right):
        return jnp.sum((left * right).reshape(-1, depth // lanes, lanes), axis=(0, 1))

    image_1 = right_side + noise_weight * finish(exchange(smoothed_spectral(first, weights)))
    sent = exchange(channel_blocks(noise_weight * image_1))
    returned = smoothed_spectral(sent, weights)
    cross = jnp.sum(sent * returned, axis=(0, 1, 2))
    cross = jnp.pad(cross, (0, lanes - cross.shape[0] % lanes if cross.shape[0] % lanes else 0))
    cross = jnp.sum(cross.reshape(-1, lanes), axis=0)
    image_norm = lane_sums(image_1, image_1)
    partials = jnp.stack(
        [lane_sums(right_side, right_side), lane_sums(right_side, image_1), image_norm, image_norm + cross]
    )
    block = chunk * local_x * local_y
    back = exchange(
        jnp.concatenate(
            [jnp.broadcast_to(partials.reshape(1, 4 * lanes), (count, 4 * lanes)), returned.reshape(count, block)],
            axis=1,
        )
    )
    image_2 = image_1 + noise_weight * finish(back[:, 4 * lanes :].reshape(count, chunk, local_x, local_y))
    summed = jnp.sum(back[:, : 4 * lanes].reshape(count, 4, lanes), axis=0)
    totals = contract("vl,lm->vm", summed, jnp.ones((lanes, lanes), jnp.float32), highest)
    moments = jnp.tile(totals, (1, depth // lanes)).reshape(4, 1, 1, depth)
    norm_0, curvature_1, image_norm, cross = moments[0], moments[1], moments[2], moments[3]
    step_1 = norm_0 / curvature_1
    norm_1 = norm_0 - 2.0 * step_1 * curvature_1 + step_1 * step_1 * image_norm
    grow = 1.0 + norm_1 / norm_0
    curvature_2 = grow * grow * curvature_1 - 2.0 * step_1 * grow * image_norm + step_1 * step_1 * cross
    step_2 = norm_1 / curvature_2
    lead = step_1 + step_2 * grow
    tail = step_2 * step_1
    solution = lead * right_side - tail * image_1
    residual = right_side - lead * image_1 + tail * image_2
    return (solution, residual)


def solution(mesh):
    return jax.shard_map(
        local,
        mesh=mesh,
        in_specs=(P("wide", "narrow", None), P("wide", "narrow", None), P("wide", "narrow", None)),
        out_specs=(P("wide", "narrow", None), P("wide", "narrow", None)),
        check_vma=False,
    )
```

```python
import math

import jax
import jax.numpy as jnp
import numpy as np
from jax import lax
from jax.sharding import PartitionSpec as P

ITERS = 2

AXES = ("wide", "narrow")

highest = lax.Precision.HIGHEST


def cas_matrix(length, columns=None):
    counter = np.arange(length, dtype=np.int64)
    frequency = counter if columns is None else np.asarray(columns, np.int64)
    phase = counter[:, None] * frequency[None, :] % length
    angle = phase.astype(np.float64) * (2.0 * math.pi / length)
    return jnp.asarray((np.cos(angle) + np.sin(angle)).astype(np.float32))


def channel_order(depth, count):
    chunk = depth // count
    if chunk % 2:
        return list(range(depth)), False
    half = chunk // 2
    order = [0, depth // 2]
    for k in range(1, half):
        order += [k, depth - k]
    for k in range(half, depth // 2):
        order += [k, depth - k]
    return order, True


def contract(spec, values, matrix):
    return jnp.einsum(spec, values, matrix, precision=highest, preferred_element_type=jnp.float32)


def exchange(blocks):
    return lax.all_to_all(blocks, AXES, 0, 0, tiled=True)


def global_sums(partials):
    count = lax.axis_size("wide") * lax.axis_size("narrow")
    spread = jnp.broadcast_to(partials[None], (count,) + partials.shape)
    return jnp.sum(exchange(spread), axis=0)


def local(sky_map, noise_weight, power_spectrum):
    local_x, local_y, depth = sky_map.shape
    n_wide = lax.axis_size("wide")
    n_narrow = lax.axis_size("narrow")
    count = n_wide * n_narrow
    chunk = depth // count
    full_x = local_x * n_wide
    full_y = local_y * n_narrow
    matrix_x = cas_matrix(full_x).reshape(n_wide, local_x, full_x)
    matrix_y = cas_matrix(full_y).reshape(n_narrow, local_y, full_y)
    order, paired = channel_order(depth, count)
    matrix_z = cas_matrix(depth, order)
    inverse_cells = 1.0 / float(full_x * full_y * depth)

    def to_planes_of(blocks, rows):
        return blocks.reshape(n_wide, n_narrow, rows, local_x, local_y)

    def to_planes(blocks):
        return to_planes_of(blocks, chunk)

    def forward_sky(planes):
        along_y = contract("wnkab,nby->wkay", planes, matrix_y)
        return contract("wkay,wax->kxy", along_y, matrix_x)

    def inverse_sky(spectral):
        along_x = contract("kxy,wax->wkay", spectral, matrix_x)
        along_y = contract("wkay,nby->wnkab", along_x, matrix_y)
        return along_y.reshape(count, chunk, local_x, local_y)

    def channel_blocks(values):
        return contract("abz,zk->kab", values, matrix_z).reshape(count, chunk, local_x, local_y)

    def finish(blocks):
        return contract("kab,zk->abz", blocks.reshape(depth, local_x, local_y), matrix_z)

    def smoothed_spectral(blocks, weights):
        return inverse_sky(forward_sky(to_planes(blocks)) * weights)

    right_side = noise_weight * sky_map

    if paired:
        half = chunk // 2
        main = jnp.transpose(power_spectrum[:, :, : depth // 2], (2, 0, 1)).reshape(
            count, half, local_x, local_y
        )
        middle = jnp.broadcast_to(
            power_spectrum[None, None, :, :, depth // 2], (count, 1, local_x, local_y)
        )
        power_blocks = jnp.concatenate([main, middle], axis=1)
        rows = half + 1
    else:
        power_blocks = jnp.transpose(power_spectrum, (2, 0, 1)).reshape(count, chunk, local_x, local_y)
        rows = chunk
    power_received = exchange(power_blocks)
    first = exchange(channel_blocks(noise_weight * right_side))
    power_planes = jnp.transpose(to_planes_of(power_received, rows), (2, 0, 3, 1, 4)).reshape(
        rows, full_x, full_y
    )
    if paired:
        device = lax.axis_index("wide") * n_narrow + lax.axis_index("narrow")
        second = jnp.where(device == 0, power_planes[half], power_planes[0])
        weights = jnp.concatenate(
            [power_planes[0:1], second[None], jnp.repeat(power_planes[1:half], 2, axis=0)], axis=0
        )
    else:
        weights = power_planes
    weights = weights * inverse_cells

    lanes = 32

    def lane_sums(left, right):
        return jnp.sum(jnp.sum(left * right, axis=(0, 1)).reshape(-1, lanes), axis=0)

    image_1 = right_side + noise_weight * finish(exchange(smoothed_spectral(first, weights)))
    sent = exchange(channel_blocks(noise_weight * image_1))
    returned = smoothed_spectral(sent, weights)
    cross = jnp.sum(sent * returned, axis=(0, 1, 2))
    cross = jnp.pad(cross, (0, lanes - cross.shape[0] % lanes if cross.shape[0] % lanes else 0))
    cross = jnp.sum(cross.reshape(-1, lanes), axis=0)
    image_norm = lane_sums(image_1, image_1)
    partials = jnp.stack(
        [lane_sums(right_side, right_side), lane_sums(right_side, image_1), image_norm, image_norm + cross]
    )
    block = chunk * local_x * local_y
    back = exchange(
        jnp.concatenate(
            [jnp.broadcast_to(partials.reshape(1, 4 * lanes), (count, 4 * lanes)), returned.reshape(count, block)],
            axis=1,
        )
    )
    image_2 = image_1 + noise_weight * finish(back[:, 4 * lanes :].reshape(count, chunk, local_x, local_y))
    summed = jnp.sum(back[:, : 4 * lanes].reshape(count, 4, lanes), axis=0)
    totals = contract("vl,lm->vm", summed, jnp.ones((lanes, depth), jnp.float32))
    moments = totals.reshape(4, 1, 1, depth)
    norm_0, curvature_1, image_norm, cross = moments[0], moments[1], moments[2], moments[3]
    step_1 = norm_0 / curvature_1
    norm_1 = norm_0 - 2.0 * step_1 * curvature_1 + step_1 * step_1 * image_norm
    grow = 1.0 + norm_1 / norm_0
    curvature_2 = grow * grow * curvature_1 - 2.0 * step_1 * grow * image_norm + step_1 * step_1 * cross
    step_2 = norm_1 / curvature_2
    lead = step_1 + step_2 * grow
    tail = step_2 * step_1
    solution = lead * right_side - tail * image_1
    residual = right_side - lead * image_1 + tail * image_2
    return (solution, residual)


def solution(mesh):
    return jax.shard_map(
        local,
        mesh=mesh,
        in_specs=(P("wide", "narrow", None), P("wide", "narrow", None), P("wide", "narrow", None)),
        out_specs=(P("wide", "narrow", None), P("wide", "narrow", None)),
        check_vma=False,
    )
```

```python
import math

import jax
import jax.numpy as jnp
import numpy as np
from jax import lax
from jax.sharding import PartitionSpec as P

ITERS = 2

AXES = ("wide", "narrow")

highest = lax.Precision.HIGHEST


def cas_matrix(length, columns=None):
    counter = np.arange(length, dtype=np.int64)
    frequency = counter if columns is None else np.asarray(columns, np.int64)
    phase = counter[:, None] * frequency[None, :] % length
    angle = phase.astype(np.float64) * (2.0 * math.pi / length)
    return jnp.asarray((np.cos(angle) + np.sin(angle)).astype(np.float32))


def channel_order(depth, count):
    chunk = depth // count
    if chunk % 2:
        return list(range(depth)), False
    half = chunk // 2
    order = [0, depth // 2]
    for k in range(1, half):
        order += [k, depth - k]
    for k in range(half, depth // 2):
        order += [k, depth - k]
    return order, True


def contract(spec, values, matrix):
    return jnp.einsum(spec, values, matrix, precision=highest, preferred_element_type=jnp.float32)


def exchange(blocks):
    size = math.prod(blocks.shape[1:])
    if size % 128:
        return lax.all_to_all(blocks, AXES, 0, 0, tiled=True)
    rows = blocks.reshape(blocks.shape[0], size // 128, 128)
    return lax.all_to_all(rows, AXES, 0, 0, tiled=True).reshape(blocks.shape)


def global_sums(partials):
    count = lax.axis_size("wide") * lax.axis_size("narrow")
    spread = jnp.broadcast_to(partials[None], (count,) + partials.shape)
    return jnp.sum(exchange(spread), axis=0)


def local(sky_map, noise_weight, power_spectrum):
    local_x, local_y, depth = sky_map.shape
    n_wide = lax.axis_size("wide")
    n_narrow = lax.axis_size("narrow")
    count = n_wide * n_narrow
    chunk = depth // count
    full_x = local_x * n_wide
    full_y = local_y * n_narrow
    matrix_x = cas_matrix(full_x).reshape(n_wide, local_x, full_x)
    matrix_y = cas_matrix(full_y).reshape(n_narrow, local_y, full_y)
    order, paired = channel_order(depth, count)
    matrix_z = cas_matrix(depth, order)
    inverse_cells = 1.0 / float(full_x * full_y * depth)

    def to_planes_of(blocks, rows):
        return blocks.reshape(n_wide, n_narrow, rows, local_x, local_y)

    def to_planes(blocks):
        return to_planes_of(blocks, chunk)

    def forward_sky(planes):
        along_y = contract("wnkab,nby->wkay", planes, matrix_y)
        return contract("wkay,wax->kxy", along_y, matrix_x)

    def inverse_sky(spectral):
        along_x = contract("kxy,wax->wkay", spectral, matrix_x)
        along_y = contract("wkay,nby->wnkab", along_x, matrix_y)
        return along_y.reshape(count, chunk, local_x, local_y)

    def channel_blocks(values):
        return contract("abz,zk->kab", values, matrix_z).reshape(count, chunk, local_x, local_y)

    def finish(blocks):
        return contract("kab,zk->abz", blocks.reshape(depth, local_x, local_y), matrix_z)

    def smoothed_spectral(blocks, weights):
        return inverse_sky(forward_sky(to_planes(blocks)) * weights)

    right_side = noise_weight * sky_map

    if paired:
        half = chunk // 2
        main = jnp.transpose(power_spectrum[:, :, : depth // 2], (2, 0, 1)).reshape(
            count, half, local_x, local_y
        )
        middle = jnp.broadcast_to(
            power_spectrum[None, None, :, :, depth // 2], (count, 1, local_x, local_y)
        )
        power_blocks = jnp.concatenate([main, middle], axis=1)
        rows = half + 1
    else:
        power_blocks = jnp.transpose(power_spectrum, (2, 0, 1)).reshape(count, chunk, local_x, local_y)
        rows = chunk
    power_received = exchange(power_blocks)
    first = exchange(channel_blocks(noise_weight * right_side))
    power_planes = jnp.transpose(to_planes_of(power_received, rows), (2, 0, 3, 1, 4)).reshape(
        rows, full_x, full_y
    )
    if paired:
        device = lax.axis_index("wide") * n_narrow + lax.axis_index("narrow")
        second = jnp.where(device == 0, power_planes[half], power_planes[0])
        weights = jnp.concatenate(
            [power_planes[0:1], second[None], jnp.repeat(power_planes[1:half], 2, axis=0)], axis=0
        )
    else:
        weights = power_planes
    weights = weights * inverse_cells

    lanes = 32

    def lane_sums(left, right):
        return jnp.sum(jnp.sum(left * right, axis=(0, 1)).reshape(-1, lanes), axis=0)

    image_1 = right_side + noise_weight * finish(exchange(smoothed_spectral(first, weights)))
    sent = exchange(channel_blocks(noise_weight * image_1))
    returned = smoothed_spectral(sent, weights)
    cross = jnp.sum(sent * returned, axis=(0, 1, 2))
    cross = jnp.pad(cross, (0, lanes - cross.shape[0] % lanes if cross.shape[0] % lanes else 0))
    cross = jnp.sum(cross.reshape(-1, lanes), axis=0)
    image_norm = lane_sums(image_1, image_1)
    partials = jnp.stack(
        [lane_sums(right_side, right_side), lane_sums(right_side, image_1), image_norm, image_norm + cross]
    )
    block = chunk * local_x * local_y
    back = exchange(
        jnp.concatenate(
            [jnp.broadcast_to(partials.reshape(1, 4 * lanes), (count, 4 * lanes)), returned.reshape(count, block)],
            axis=1,
        )
    )
    image_2 = image_1 + noise_weight * finish(back[:, 4 * lanes :].reshape(count, chunk, local_x, local_y))
    summed = jnp.sum(back[:, : 4 * lanes].reshape(count, 4, lanes), axis=0)
    totals = contract("vl,lm->vm", summed, jnp.ones((lanes, depth), jnp.float32))
    moments = totals.reshape(4, 1, 1, depth)
    norm_0, curvature_1, image_norm, cross = moments[0], moments[1], moments[2], moments[3]
    step_1 = norm_0 / curvature_1
    norm_1 = norm_0 - 2.0 * step_1 * curvature_1 + step_1 * step_1 * image_norm
    grow = 1.0 + norm_1 / norm_0
    curvature_2 = grow * grow * curvature_1 - 2.0 * step_1 * grow * image_norm + step_1 * step_1 * cross
    step_2 = norm_1 / curvature_2
    lead = step_1 + step_2 * grow
    tail = step_2 * step_1
    solution = lead * right_side - tail * image_1
    residual = right_side - lead * image_1 + tail * image_2
    return (solution, residual)


def solution(mesh):
    return jax.shard_map(
        local,
        mesh=mesh,
        in_specs=(P("wide", "narrow", None), P("wide", "narrow", None), P("wide", "narrow", None)),
        out_specs=(P("wide", "narrow", None), P("wide", "narrow", None)),
        check_vma=False,
    )
```

```python
import math

import jax
import jax.numpy as jnp
import numpy as np
from jax import lax
from jax.sharding import PartitionSpec as P

ITERS = 2

AXES = ("wide", "narrow")

highest = lax.Precision.HIGHEST


def cas_matrix(length, columns=None):
    counter = np.arange(length, dtype=np.int64)
    frequency = counter if columns is None else np.asarray(columns, np.int64)
    phase = counter[:, None] * frequency[None, :] % length
    angle = phase.astype(np.float64) * (2.0 * math.pi / length)
    return jnp.asarray((np.cos(angle) + np.sin(angle)).astype(np.float32))


def channel_order(depth, count):
    chunk = depth // count
    if chunk % 2:
        return list(range(depth)), False
    half = chunk // 2
    order = [0, depth // 2]
    for k in range(1, half):
        order += [k, depth - k]
    for k in range(half, depth // 2):
        order += [k, depth - k]
    return order, True


def contract(spec, values, matrix):
    return jnp.einsum(spec, values, matrix, precision=highest, preferred_element_type=jnp.float32)


def exchange(blocks):
    return lax.all_to_all(blocks, AXES, 0, 0, tiled=True)


def global_sums(partials):
    count = lax.axis_size("wide") * lax.axis_size("narrow")
    spread = jnp.broadcast_to(partials[None], (count,) + partials.shape)
    return jnp.sum(exchange(spread), axis=0)


def local(sky_map, noise_weight, power_spectrum):
    local_x, local_y, depth = sky_map.shape
    n_wide = lax.axis_size("wide")
    n_narrow = lax.axis_size("narrow")
    count = n_wide * n_narrow
    chunk = depth // count
    full_x = local_x * n_wide
    full_y = local_y * n_narrow
    matrix_x = cas_matrix(full_x).reshape(n_wide, local_x, full_x)
    matrix_y = cas_matrix(full_y).reshape(n_narrow, local_y, full_y)
    order, paired = channel_order(depth, count)
    matrix_z = cas_matrix(depth, order)
    inverse_cells = 1.0 / float(full_x * full_y * depth)

    def to_planes_of(blocks, rows):
        return blocks.reshape(n_wide, n_narrow, rows, local_x, local_y)

    def to_planes(blocks):
        return to_planes_of(blocks, chunk)

    def forward_sky(planes):
        along_y = contract("wnkab,nby->wkay", planes, matrix_y)
        return contract("wkay,wax->kxy", along_y, matrix_x)

    def inverse_sky(spectral):
        along_x = contract("kxy,wax->wkay", spectral, matrix_x)
        along_y = contract("wkay,nby->wnkab", along_x, matrix_y)
        return along_y.reshape(count, chunk, local_x, local_y)

    def channel_blocks(values):
        return contract("abz,zk->kab", values, matrix_z).reshape(count, chunk, local_x, local_y)

    def finish(blocks):
        return contract("kab,zk->abz", blocks.reshape(depth, local_x, local_y), matrix_z)

    def smoothed_spectral(blocks, weights):
        return inverse_sky(forward_sky(to_planes(blocks)) * weights)

    right_side = noise_weight * sky_map

    if paired:
        half = chunk // 2
        rows = half + 1
        picked = []
        for d in range(count):
            picked += list(range(d * half, (d + 1) * half)) + [depth // 2]
    else:
        rows = chunk
        picked = list(range(depth))
    selection = np.zeros((depth, count * rows), np.float32)
    selection[picked, np.arange(count * rows)] = 1.0
    power_blocks = contract("abz,zr->rab", power_spectrum, jnp.asarray(selection)).reshape(
        count, rows, local_x, local_y
    )
    power_received = exchange(power_blocks)
    first = exchange(channel_blocks(noise_weight * right_side))
    power_planes = jnp.transpose(to_planes_of(power_received, rows), (2, 0, 3, 1, 4)).reshape(
        rows, full_x, full_y
    )
    if paired:
        device = lax.axis_index("wide") * n_narrow + lax.axis_index("narrow")
        second = jnp.where(device == 0, power_planes[half], power_planes[0])
        weights = jnp.concatenate(
            [power_planes[0:1], second[None], jnp.repeat(power_planes[1:half], 2, axis=0)], axis=0
        )
    else:
        weights = power_planes
    weights = weights * inverse_cells

    lanes = 32

    def lane_sums(left, right):
        return jnp.sum(jnp.sum(left * right, axis=(0, 1)).reshape(-1, lanes), axis=0)

    image_1 = right_side + noise_weight * finish(exchange(smoothed_spectral(first, weights)))
    sent = exchange(channel_blocks(noise_weight * image_1))
    returned = smoothed_spectral(sent, weights)
    cross = jnp.sum(sent * returned, axis=(0, 1, 2))
    cross = jnp.pad(cross, (0, lanes - cross.shape[0] % lanes if cross.shape[0] % lanes else 0))
    cross = jnp.sum(cross.reshape(-1, lanes), axis=0)
    image_norm = lane_sums(image_1, image_1)
    partials = jnp.stack(
        [lane_sums(right_side, right_side), lane_sums(right_side, image_1), image_norm, image_norm + cross]
    )
    block = chunk * local_x * local_y
    back = exchange(
        jnp.concatenate(
            [jnp.broadcast_to(partials.reshape(1, 4 * lanes), (count, 4 * lanes)), returned.reshape(count, block)],
            axis=1,
        )
    )
    image_2 = image_1 + noise_weight * finish(back[:, 4 * lanes :].reshape(count, chunk, local_x, local_y))
    summed = jnp.sum(back[:, : 4 * lanes].reshape(count, 4, lanes), axis=0)
    totals = contract("vl,lm->vm", summed, jnp.ones((lanes, depth), jnp.float32))
    moments = totals.reshape(4, 1, 1, depth)
    norm_0, curvature_1, image_norm, cross = moments[0], moments[1], moments[2], moments[3]
    step_1 = norm_0 / curvature_1
    norm_1 = norm_0 - 2.0 * step_1 * curvature_1 + step_1 * step_1 * image_norm
    grow = 1.0 + norm_1 / norm_0
    curvature_2 = grow * grow * curvature_1 - 2.0 * step_1 * grow * image_norm + step_1 * step_1 * cross
    step_2 = norm_1 / curvature_2
    lead = step_1 + step_2 * grow
    tail = step_2 * step_1
    solution = lead * right_side - tail * image_1
    residual = right_side - lead * image_1 + tail * image_2
    return (solution, residual)


def solution(mesh):
    return jax.shard_map(
        local,
        mesh=mesh,
        in_specs=(P("wide", "narrow", None), P("wide", "narrow", None), P("wide", "narrow", None)),
        out_specs=(P("wide", "narrow", None), P("wide", "narrow", None)),
        check_vma=False,
    )
```

```python
import math

import jax
import jax.numpy as jnp
import numpy as np
from jax import lax
from jax.sharding import PartitionSpec as P

ITERS = 2

AXES = ("wide", "narrow")

highest = lax.Precision.HIGHEST


def cas_matrix(length, columns=None):
    counter = np.arange(length, dtype=np.int64)
    frequency = counter if columns is None else np.asarray(columns, np.int64)
    phase = counter[:, None] * frequency[None, :] % length
    angle = phase.astype(np.float64) * (2.0 * math.pi / length)
    return jnp.asarray((np.cos(angle) + np.sin(angle)).astype(np.float32))


def channel_order(depth, count):
    chunk = depth // count
    if chunk % 2:
        return list(range(depth)), False
    half = chunk // 2
    order = [0, depth // 2]
    for k in range(1, half):
        order += [k, depth - k]
    for k in range(half, depth // 2):
        order += [k, depth - k]
    return order, True


def contract(spec, values, matrix):
    return jnp.einsum(spec, values, matrix, precision=highest, preferred_element_type=jnp.float32)


def exchange(blocks):
    return lax.all_to_all(blocks, AXES, 0, 0, tiled=True)


def global_sums(partials):
    count = lax.axis_size("wide") * lax.axis_size("narrow")
    spread = jnp.broadcast_to(partials[None], (count,) + partials.shape)
    return jnp.sum(exchange(spread), axis=0)


def local(sky_map, noise_weight, power_spectrum):
    local_x, local_y, depth = sky_map.shape
    n_wide = lax.axis_size("wide")
    n_narrow = lax.axis_size("narrow")
    count = n_wide * n_narrow
    chunk = depth // count
    full_x = local_x * n_wide
    full_y = local_y * n_narrow
    matrix_x = cas_matrix(full_x).reshape(n_wide, local_x, full_x)
    matrix_y = cas_matrix(full_y).reshape(n_narrow, local_y, full_y)
    order, paired = channel_order(depth, count)
    matrix_z = cas_matrix(depth, order)
    inverse_cells = 1.0 / float(full_x * full_y * depth)

    def to_planes_of(blocks, rows):
        return blocks.reshape(n_wide, n_narrow, rows, local_x, local_y)

    def to_planes(blocks):
        return to_planes_of(blocks, chunk)

    def forward_sky(planes):
        along_y = contract("wnkab,nby->wkay", planes, matrix_y)
        return contract("wkay,wax->kxy", along_y, matrix_x)

    def inverse_sky(spectral):
        along_x = contract("kxy,wax->wkay", spectral, matrix_x)
        along_y = contract("wkay,nby->wnkab", along_x, matrix_y)
        return along_y.reshape(count, chunk, local_x, local_y)

    def channel_blocks(values):
        return contract("abz,zk->kab", values, matrix_z).reshape(count, chunk, local_x, local_y)

    def finish(blocks):
        return contract("kab,zk->abz", blocks.reshape(depth, local_x, local_y), matrix_z)

    def smoothed_spectral(blocks, weights):
        return inverse_sky(forward_sky(to_planes(blocks)) * weights)

    right_side = noise_weight * sky_map

    if paired:
        half = chunk // 2
        main = jnp.transpose(power_spectrum[:, :, : depth // 2], (2, 0, 1)).reshape(
            count, half, local_x, local_y
        )
        middle = jnp.broadcast_to(
            power_spectrum[None, None, :, :, depth // 2], (count, 1, local_x, local_y)
        )
        power_blocks = jnp.concatenate([main, middle], axis=1)
        rows = half + 1
    else:
        power_blocks = jnp.transpose(power_spectrum, (2, 0, 1)).reshape(count, chunk, local_x, local_y)
        rows = chunk
    power_received = exchange(power_blocks)
    first = exchange(channel_blocks(noise_weight * right_side))
    power_planes = jnp.transpose(to_planes_of(power_received, rows), (2, 0, 3, 1, 4)).reshape(
        rows, full_x, full_y
    )
    if paired:
        device = lax.axis_index("wide") * n_narrow + lax.axis_index("narrow")
        second = jnp.where(device == 0, power_planes[half], power_planes[0])
        weights = jnp.concatenate(
            [power_planes[0:1], second[None], jnp.repeat(power_planes[1:half], 2, axis=0)], axis=0
        )
    else:
        weights = power_planes
    weights = weights * inverse_cells

    lanes = 32

    def lane_sums(left, right):
        return jnp.sum(jnp.sum(left * right, axis=(0, 1)).reshape(-1, lanes), axis=0)

    image_1 = right_side + noise_weight * finish(exchange(smoothed_spectral(first, weights)))
    sent = exchange(channel_blocks(noise_weight * image_1))
    returned = smoothed_spectral(sent, weights)
    cross = jnp.sum(sent * returned, axis=(0, 1, 2))
    cross = jnp.pad(cross, (0, lanes - cross.shape[0] % lanes if cross.shape[0] % lanes else 0))
    cross = jnp.sum(cross.reshape(-1, lanes), axis=0)
    image_norm = lane_sums(image_1, image_1)
    partials = jnp.stack(
        [lane_sums(right_side, right_side), lane_sums(right_side, image_1), image_norm, image_norm + cross]
    )
    block = chunk * local_x * local_y
    back = exchange(
        jnp.concatenate(
            [returned.reshape(count, block), jnp.broadcast_to(partials.reshape(1, 4 * lanes), (count, 4 * lanes))],
            axis=1,
        )
    )
    image_2 = image_1 + noise_weight * finish(back[:, :block].reshape(count, chunk, local_x, local_y))
    summed = jnp.sum(back[:, block:].reshape(count, 4, lanes), axis=0)
    totals = contract("vl,lm->vm", summed, jnp.ones((lanes, depth), jnp.float32))
    moments = totals.reshape(4, 1, 1, depth)
    norm_0, curvature_1, image_norm, cross = moments[0], moments[1], moments[2], moments[3]
    step_1 = norm_0 / curvature_1
    norm_1 = norm_0 - 2.0 * step_1 * curvature_1 + step_1 * step_1 * image_norm
    grow = 1.0 + norm_1 / norm_0
    curvature_2 = grow * grow * curvature_1 - 2.0 * step_1 * grow * image_norm + step_1 * step_1 * cross
    step_2 = norm_1 / curvature_2
    lead = step_1 + step_2 * grow
    tail = step_2 * step_1
    solution = lead * right_side - tail * image_1
    residual = right_side - lead * image_1 + tail * image_2
    return (solution, residual)


def solution(mesh):
    return jax.shard_map(
        local,
        mesh=mesh,
        in_specs=(P("wide", "narrow", None), P("wide", "narrow", None), P("wide", "narrow", None)),
        out_specs=(P("wide", "narrow", None), P("wide", "narrow", None)),
        check_vma=False,
    )
```

```python
import math

import jax
import jax.numpy as jnp
import numpy as np
from jax import lax
from jax.sharding import PartitionSpec as P

ITERS = 2

AXES = ("wide", "narrow")

highest = lax.Precision.HIGHEST


def cas_matrix(length, columns=None):
    counter = np.arange(length, dtype=np.int64)
    frequency = counter if columns is None else np.asarray(columns, np.int64)
    phase = counter[:, None] * frequency[None, :] % length
    angle = phase.astype(np.float64) * (2.0 * math.pi / length)
    return jnp.asarray((np.cos(angle) + np.sin(angle)).astype(np.float32))


def channel_order(depth, count):
    chunk = depth // count
    if chunk % 2:
        return list(range(depth)), False
    half = chunk // 2
    order = [0, depth // 2]
    for k in range(1, half):
        order += [k, depth - k]
    for k in range(half, depth // 2):
        order += [k, depth - k]
    return order, True


def contract(spec, values, matrix):
    return jnp.einsum(spec, values, matrix, precision=highest, preferred_element_type=jnp.float32)


def exchange(blocks):
    return lax.all_to_all(blocks, AXES, 0, 0, tiled=True)


def global_sums(partials):
    count = lax.axis_size("wide") * lax.axis_size("narrow")
    spread = jnp.broadcast_to(partials[None], (count,) + partials.shape)
    return jnp.sum(exchange(spread), axis=0)


def local(sky_map, noise_weight, power_spectrum):
    local_x, local_y, depth = sky_map.shape
    n_wide = lax.axis_size("wide")
    n_narrow = lax.axis_size("narrow")
    count = n_wide * n_narrow
    chunk = depth // count
    full_x = local_x * n_wide
    full_y = local_y * n_narrow
    matrix_x = cas_matrix(full_x).reshape(n_wide, local_x, full_x)
    matrix_y = cas_matrix(full_y).reshape(n_narrow, local_y, full_y)
    order, paired = channel_order(depth, count)
    matrix_z = cas_matrix(depth, order)
    inverse_cells = 1.0 / float(full_x * full_y * depth)

    def to_planes_of(blocks, rows):
        return blocks.reshape(n_wide, n_narrow, rows, local_x, local_y)

    def to_planes(blocks):
        return blocks.reshape(n_wide, n_narrow, local_x, chunk, local_y)

    def forward_sky(planes):
        along_y = contract("wnakb,nby->wkay", planes, matrix_y)
        return contract("wkay,wax->kxy", along_y, matrix_x)

    def inverse_sky(spectral):
        along_x = contract("kxy,wax->wkay", spectral, matrix_x)
        along_y = contract("wkay,nby->wnakb", along_x, matrix_y)
        return along_y.reshape(count, local_x, chunk, local_y)

    def channel_blocks(values):
        return contract("abz,zdk->dakb", values, matrix_z.reshape(depth, count, chunk))

    def finish(blocks):
        return contract("dakb,zdk->abz", blocks, matrix_z.reshape(depth, count, chunk))

    def smoothed_spectral(blocks, weights):
        return inverse_sky(forward_sky(to_planes(blocks)) * weights)

    right_side = noise_weight * sky_map

    if paired:
        half = chunk // 2
        main = jnp.transpose(power_spectrum[:, :, : depth // 2], (2, 0, 1)).reshape(
            count, half, local_x, local_y
        )
        middle = jnp.broadcast_to(
            power_spectrum[None, None, :, :, depth // 2], (count, 1, local_x, local_y)
        )
        power_blocks = jnp.concatenate([main, middle], axis=1)
        rows = half + 1
    else:
        power_blocks = jnp.transpose(power_spectrum, (2, 0, 1)).reshape(count, chunk, local_x, local_y)
        rows = chunk
    power_received = exchange(power_blocks)
    first = exchange(channel_blocks(noise_weight * right_side))
    power_planes = jnp.transpose(to_planes_of(power_received, rows), (2, 0, 3, 1, 4)).reshape(
        rows, full_x, full_y
    )
    if paired:
        device = lax.axis_index("wide") * n_narrow + lax.axis_index("narrow")
        second = jnp.where(device == 0, power_planes[half], power_planes[0])
        weights = jnp.concatenate(
            [power_planes[0:1], second[None], jnp.repeat(power_planes[1:half], 2, axis=0)], axis=0
        )
    else:
        weights = power_planes
    weights = weights * inverse_cells

    lanes = 32

    def lane_sums(left, right):
        return jnp.sum(jnp.sum(left * right, axis=(0, 1)).reshape(-1, lanes), axis=0)

    image_1 = right_side + noise_weight * finish(exchange(smoothed_spectral(first, weights)))
    sent = exchange(channel_blocks(noise_weight * image_1))
    returned = smoothed_spectral(sent, weights)
    cross = jnp.sum(sent * returned, axis=(0, 1, 2))
    cross = jnp.pad(cross, (0, lanes - cross.shape[0] % lanes if cross.shape[0] % lanes else 0))
    cross = jnp.sum(cross.reshape(-1, lanes), axis=0)
    image_norm = lane_sums(image_1, image_1)
    partials = jnp.stack(
        [lane_sums(right_side, right_side), lane_sums(right_side, image_1), image_norm, image_norm + cross]
    )
    block = chunk * local_x * local_y
    back = exchange(
        jnp.concatenate(
            [jnp.broadcast_to(partials.reshape(1, 4 * lanes), (count, 4 * lanes)), returned.reshape(count, block)],
            axis=1,
        )
    )
    image_2 = image_1 + noise_weight * finish(back[:, 4 * lanes :].reshape(count, local_x, chunk, local_y))
    summed = jnp.sum(back[:, : 4 * lanes].reshape(count, 4, lanes), axis=0)
    totals = contract("vl,lm->vm", summed, jnp.ones((lanes, depth), jnp.float32))
    moments = totals.reshape(4, 1, 1, depth)
    norm_0, curvature_1, image_norm, cross = moments[0], moments[1], moments[2], moments[3]
    step_1 = norm_0 / curvature_1
    norm_1 = norm_0 - 2.0 * step_1 * curvature_1 + step_1 * step_1 * image_norm
    grow = 1.0 + norm_1 / norm_0
    curvature_2 = grow * grow * curvature_1 - 2.0 * step_1 * grow * image_norm + step_1 * step_1 * cross
    step_2 = norm_1 / curvature_2
    lead = step_1 + step_2 * grow
    tail = step_2 * step_1
    solution = lead * right_side - tail * image_1
    residual = right_side - lead * image_1 + tail * image_2
    return (solution, residual)


def solution(mesh):
    return jax.shard_map(
        local,
        mesh=mesh,
        in_specs=(P("wide", "narrow", None), P("wide", "narrow", None), P("wide", "narrow", None)),
        out_specs=(P("wide", "narrow", None), P("wide", "narrow", None)),
        check_vma=False,
    )
```

```python
import math

import jax
import jax.numpy as jnp
import numpy as np
from jax import lax
from jax.sharding import PartitionSpec as P

ITERS = 2

AXES = ("wide", "narrow")

highest = lax.Precision.HIGHEST


def cas_matrix(length, columns=None):
    counter = np.arange(length, dtype=np.int64)
    frequency = counter if columns is None else np.asarray(columns, np.int64)
    phase = counter[:, None] * frequency[None, :] % length
    angle = phase.astype(np.float64) * (2.0 * math.pi / length)
    return jnp.asarray((np.cos(angle) + np.sin(angle)).astype(np.float32))


def channel_order(depth, count):
    chunk = depth // count
    if chunk % 2:
        return list(range(depth)), False
    half = chunk // 2
    order = [0, depth // 2]
    for k in range(1, half):
        order += [k, depth - k]
    for k in range(half, depth // 2):
        order += [k, depth - k]
    return order, True


def contract(spec, values, matrix):
    return jnp.einsum(spec, values, matrix, precision=highest, preferred_element_type=jnp.float32)


def exchange(blocks):
    return lax.all_to_all(blocks, AXES, 0, 0, tiled=True)


def global_sums(partials):
    count = lax.axis_size("wide") * lax.axis_size("narrow")
    spread = jnp.broadcast_to(partials[None], (count,) + partials.shape)
    return jnp.sum(exchange(spread), axis=0)


def local(sky_map, noise_weight, power_spectrum):
    local_x, local_y, depth = sky_map.shape
    n_wide = lax.axis_size("wide")
    n_narrow = lax.axis_size("narrow")
    count = n_wide * n_narrow
    chunk = depth // count
    full_x = local_x * n_wide
    full_y = local_y * n_narrow
    matrix_x = cas_matrix(full_x).reshape(n_wide, local_x, full_x)
    matrix_y = cas_matrix(full_y).reshape(n_narrow, local_y, full_y)
    order, paired = channel_order(depth, count)
    matrix_z = cas_matrix(depth, order)
    inverse_cells = 1.0 / float(full_x * full_y * depth)

    def to_planes_of(blocks, rows):
        return blocks.reshape(n_wide, n_narrow, rows, local_x, local_y)

    def to_planes(blocks):
        return blocks.reshape(n_wide, n_narrow, local_x, chunk, local_y)

    def forward_sky(planes):
        along_y = contract("wnakb,nby->wkay", planes, matrix_y)
        return contract("wkay,wax->kxy", along_y, matrix_x)

    def inverse_sky(spectral):
        along_x = contract("kxy,wax->wkay", spectral, matrix_x)
        along_y = contract("wkay,nby->wnakb", along_x, matrix_y)
        return along_y.reshape(count, local_x, chunk, local_y)

    def channel_blocks(values):
        return contract("abz,zdk->dakb", values, matrix_z.reshape(depth, count, chunk))

    def finish(blocks):
        return contract("dakb,zdk->abz", blocks, matrix_z.reshape(depth, count, chunk))

    def smoothed_spectral(blocks, weights):
        return inverse_sky(forward_sky(to_planes(blocks)) * weights)

    right_side = noise_weight * sky_map

    if paired:
        half = chunk // 2
        main = jnp.transpose(power_spectrum[:, :, : depth // 2], (2, 0, 1)).reshape(
            count, half, local_x, local_y
        )
        middle = jnp.broadcast_to(
            power_spectrum[None, None, :, :, depth // 2], (count, 1, local_x, local_y)
        )
        power_blocks = jnp.concatenate([main, middle], axis=1)
        rows = half + 1
    else:
        power_blocks = jnp.transpose(power_spectrum, (2, 0, 1)).reshape(count, chunk, local_x, local_y)
        rows = chunk
    power_received = exchange(power_blocks)
    first = exchange(channel_blocks(noise_weight * right_side))
    power_planes = jnp.transpose(to_planes_of(power_received, rows), (2, 0, 3, 1, 4)).reshape(
        rows, full_x, full_y
    )
    if paired:
        device = lax.axis_index("wide") * n_narrow + lax.axis_index("narrow")
        second = jnp.where(device == 0, power_planes[half], power_planes[0])
        weights = jnp.concatenate(
            [power_planes[0:1], second[None], jnp.repeat(power_planes[1:half], 2, axis=0)], axis=0
        )
    else:
        weights = power_planes
    weights = weights * inverse_cells

    lanes = 32

    def lane_sums(left, right):
        return jnp.sum(jnp.sum(left * right, axis=(0, 1)).reshape(-1, lanes), axis=0)

    image_1 = right_side + noise_weight * finish(exchange(smoothed_spectral(first, weights)))
    sent = exchange(channel_blocks(noise_weight * image_1))
    returned = smoothed_spectral(sent, weights)
    cross = jnp.sum(sent * returned, axis=(0, 1, 2))
    cross = jnp.pad(cross, (0, lanes - cross.shape[0] % lanes if cross.shape[0] % lanes else 0))
    cross = jnp.sum(cross.reshape(-1, lanes), axis=0)
    image_norm = lane_sums(image_1, image_1)
    partials = jnp.stack(
        [lane_sums(right_side, right_side), lane_sums(right_side, image_1), image_norm, image_norm + cross]
    )
    row = chunk * local_y
    extra = -(-4 * lanes // row)
    tail_rows = jnp.pad(partials.reshape(-1), (0, extra * row - 4 * lanes)).reshape(1, extra, chunk, local_y)
    back = exchange(
        jnp.concatenate([returned, jnp.broadcast_to(tail_rows, (count, extra, chunk, local_y))], axis=1)
    )
    image_2 = image_1 + noise_weight * finish(back[:, :local_x])
    summed = jnp.sum(back[:, local_x:].reshape(count, -1)[:, : 4 * lanes].reshape(count, 4, lanes), axis=0)
    totals = contract("vl,lm->vm", summed, jnp.ones((lanes, depth), jnp.float32))
    moments = totals.reshape(4, 1, 1, depth)
    norm_0, curvature_1, image_norm, cross = moments[0], moments[1], moments[2], moments[3]
    step_1 = norm_0 / curvature_1
    norm_1 = norm_0 - 2.0 * step_1 * curvature_1 + step_1 * step_1 * image_norm
    grow = 1.0 + norm_1 / norm_0
    curvature_2 = grow * grow * curvature_1 - 2.0 * step_1 * grow * image_norm + step_1 * step_1 * cross
    step_2 = norm_1 / curvature_2
    lead = step_1 + step_2 * grow
    tail = step_2 * step_1
    solution = lead * right_side - tail * image_1
    residual = right_side - lead * image_1 + tail * image_2
    return (solution, residual)


def solution(mesh):
    return jax.shard_map(
        local,
        mesh=mesh,
        in_specs=(P("wide", "narrow", None), P("wide", "narrow", None), P("wide", "narrow", None)),
        out_specs=(P("wide", "narrow", None), P("wide", "narrow", None)),
        check_vma=False,
    )
```

```python
import math

import jax
import jax.numpy as jnp
import numpy as np
from jax import lax
from jax.sharding import PartitionSpec as P

ITERS = 2

AXES = ("wide", "narrow")

highest = lax.Precision.HIGHEST


def cas_matrix(length, columns=None):
    counter = np.arange(length, dtype=np.int64)
    frequency = counter if columns is None else np.asarray(columns, np.int64)
    phase = counter[:, None] * frequency[None, :] % length
    angle = phase.astype(np.float64) * (2.0 * math.pi / length)
    return jnp.asarray((np.cos(angle) + np.sin(angle)).astype(np.float32))


def channel_order(depth, count):
    chunk = depth // count
    if chunk % 2:
        return list(range(depth)), False
    half = chunk // 2
    order = [0, depth // 2]
    for k in range(1, half):
        order += [k, depth - k]
    for k in range(half, depth // 2):
        order += [k, depth - k]
    return order, True


def contract(spec, values, matrix):
    return jnp.einsum(spec, values, matrix, precision=highest, preferred_element_type=jnp.float32)


def exchange(blocks):
    return lax.all_to_all(blocks, AXES, 0, 0, tiled=True)


def global_sums(partials):
    count = lax.axis_size("wide") * lax.axis_size("narrow")
    spread = jnp.broadcast_to(partials[None], (count,) + partials.shape)
    return jnp.sum(exchange(spread), axis=0)


def local(sky_map, noise_weight, power_spectrum):
    local_x, local_y, depth = sky_map.shape
    n_wide = lax.axis_size("wide")
    n_narrow = lax.axis_size("narrow")
    count = n_wide * n_narrow
    chunk = depth // count
    full_x = local_x * n_wide
    full_y = local_y * n_narrow
    matrix_x = cas_matrix(full_x).reshape(n_wide, local_x, full_x)
    matrix_y = cas_matrix(full_y).reshape(n_narrow, local_y, full_y)
    order, paired = channel_order(depth, count)
    matrix_z = cas_matrix(depth, order)
    inverse_cells = 1.0 / float(full_x * full_y * depth)

    def to_planes_of(blocks, rows):
        return blocks.reshape(n_wide, n_narrow, local_x, rows, local_y)

    def to_planes(blocks):
        return to_planes_of(blocks, chunk)

    def forward_sky(planes):
        along_y = contract("wnakb,nby->wkay", planes, matrix_y)
        return contract("wkay,wax->kxy", along_y, matrix_x)

    def inverse_sky(spectral):
        along_x = contract("kxy,wax->wkay", spectral, matrix_x)
        along_y = contract("wkay,nby->wnakb", along_x, matrix_y)
        return along_y.reshape(count, local_x, chunk, local_y)

    def channel_blocks(values):
        return contract("abz,zdk->dakb", values, matrix_z.reshape(depth, count, chunk))

    def finish(blocks):
        return contract("dakb,zdk->abz", blocks, matrix_z.reshape(depth, count, chunk))

    def smoothed_spectral(blocks, weights):
        return inverse_sky(forward_sky(to_planes(blocks)) * weights)

    right_side = noise_weight * sky_map

    if paired:
        half = chunk // 2
        main = jnp.transpose(
            power_spectrum[:, :, : depth // 2].reshape(local_x, local_y, count, half), (2, 0, 3, 1)
        )
        middle = jnp.broadcast_to(
            power_spectrum[None, :, None, :, depth // 2], (count, local_x, 1, local_y)
        )
        power_blocks = jnp.concatenate([main, middle], axis=2)
        rows = half + 1
    else:
        power_blocks = jnp.transpose(power_spectrum.reshape(local_x, local_y, count, chunk), (2, 0, 3, 1))
        rows = chunk
    power_received = exchange(power_blocks)
    first = exchange(channel_blocks(noise_weight * right_side))
    power_planes = jnp.transpose(to_planes_of(power_received, rows), (3, 0, 2, 1, 4)).reshape(
        rows, full_x, full_y
    )
    if paired:
        device = lax.axis_index("wide") * n_narrow + lax.axis_index("narrow")
        second = jnp.where(device == 0, power_planes[half], power_planes[0])
        weights = jnp.concatenate(
            [power_planes[0:1], second[None], jnp.repeat(power_planes[1:half], 2, axis=0)], axis=0
        )
    else:
        weights = power_planes
    weights = weights * inverse_cells

    lanes = 32

    def lane_sums(left, right):
        return jnp.sum(jnp.sum(left * right, axis=(0, 1)).reshape(-1, lanes), axis=0)

    image_1 = right_side + noise_weight * finish(exchange(smoothed_spectral(first, weights)))
    sent = exchange(channel_blocks(noise_weight * image_1))
    returned = smoothed_spectral(sent, weights)
    cross = jnp.sum(sent * returned, axis=(0, 1, 2))
    cross = jnp.pad(cross, (0, lanes - cross.shape[0] % lanes if cross.shape[0] % lanes else 0))
    cross = jnp.sum(cross.reshape(-1, lanes), axis=0)
    image_norm = lane_sums(image_1, image_1)
    partials = jnp.stack(
        [lane_sums(right_side, right_side), lane_sums(right_side, image_1), image_norm, image_norm + cross]
    )
    block = chunk * local_x * local_y
    back = exchange(
        jnp.concatenate(
            [jnp.broadcast_to(partials.reshape(1, 4 * lanes), (count, 4 * lanes)), returned.reshape(count, block)],
            axis=1,
        )
    )
    image_2 = image_1 + noise_weight * finish(back[:, 4 * lanes :].reshape(count, local_x, chunk, local_y))
    summed = jnp.sum(back[:, : 4 * lanes].reshape(count, 4, lanes), axis=0)
    totals = contract("vl,lm->vm", summed, jnp.ones((lanes, depth), jnp.float32))
    moments = totals.reshape(4, 1, 1, depth)
    norm_0, curvature_1, image_norm, cross = moments[0], moments[1], moments[2], moments[3]
    step_1 = norm_0 / curvature_1
    norm_1 = norm_0 - 2.0 * step_1 * curvature_1 + step_1 * step_1 * image_norm
    grow = 1.0 + norm_1 / norm_0
    curvature_2 = grow * grow * curvature_1 - 2.0 * step_1 * grow * image_norm + step_1 * step_1 * cross
    step_2 = norm_1 / curvature_2
    lead = step_1 + step_2 * grow
    tail = step_2 * step_1
    solution = lead * right_side - tail * image_1
    residual = right_side - lead * image_1 + tail * image_2
    return (solution, residual)


def solution(mesh):
    return jax.shard_map(
        local,
        mesh=mesh,
        in_specs=(P("wide", "narrow", None), P("wide", "narrow", None), P("wide", "narrow", None)),
        out_specs=(P("wide", "narrow", None), P("wide", "narrow", None)),
        check_vma=False,
    )
```

```python
import math

import jax
import jax.numpy as jnp
import numpy as np
from jax import lax
from jax.sharding import PartitionSpec as P

ITERS = 2

AXES = ("wide", "narrow")

highest = lax.Precision.HIGHEST


def cas_matrix(length, columns=None):
    counter = np.arange(length, dtype=np.int64)
    frequency = counter if columns is None else np.asarray(columns, np.int64)
    phase = counter[:, None] * frequency[None, :] % length
    angle = phase.astype(np.float64) * (2.0 * math.pi / length)
    return jnp.asarray((np.cos(angle) + np.sin(angle)).astype(np.float32))


def channel_order(depth, count):
    chunk = depth // count
    if chunk % 2:
        return list(range(depth)), False
    half = chunk // 2
    order = [0, depth // 2]
    for k in range(1, half):
        order += [k, depth - k]
    for k in range(half, depth // 2):
        order += [k, depth - k]
    return order, True


def contract(spec, values, matrix):
    return jnp.einsum(spec, values, matrix, precision=highest, preferred_element_type=jnp.float32)


def exchange(blocks):
    return lax.all_to_all(blocks, AXES, 0, 0, tiled=True)


def global_sums(partials):
    count = lax.axis_size("wide") * lax.axis_size("narrow")
    spread = jnp.broadcast_to(partials[None], (count,) + partials.shape)
    return jnp.sum(exchange(spread), axis=0)


def local(sky_map, noise_weight, power_spectrum):
    local_x, local_y, depth = sky_map.shape
    n_wide = lax.axis_size("wide")
    n_narrow = lax.axis_size("narrow")
    count = n_wide * n_narrow
    chunk = depth // count
    full_x = local_x * n_wide
    full_y = local_y * n_narrow
    matrix_x = cas_matrix(full_x).reshape(n_wide, local_x, full_x)
    matrix_y = cas_matrix(full_y).reshape(n_narrow, local_y, full_y)
    order, paired = channel_order(depth, count)
    matrix_z = cas_matrix(depth, order)
    inverse_cells = 1.0 / float(full_x * full_y * depth)

    def to_planes_of(blocks, rows):
        return blocks.reshape(n_wide, n_narrow, rows, local_x, local_y)

    def to_planes(blocks):
        return blocks.reshape(n_wide, n_narrow, local_x, chunk, local_y)

    def forward_sky(planes):
        along_y = contract("wnakb,nby->wkay", planes, matrix_y)
        return contract("wkay,wax->kxy", along_y, matrix_x)

    def inverse_sky(spectral):
        along_x = contract("kxy,wax->wkay", spectral, matrix_x)
        along_y = contract("wkay,nby->wnakb", along_x, matrix_y)
        return along_y.reshape(count, local_x, chunk, local_y)

    def channel_blocks(values):
        return contract("abz,zdk->dakb", values, matrix_z.reshape(depth, count, chunk))

    def finish(blocks):
        return contract("dakb,zdk->abz", blocks, matrix_z.reshape(depth, count, chunk))

    def smoothed_spectral(blocks, weights):
        return inverse_sky(forward_sky(to_planes(blocks)) * weights)

    right_side = noise_weight * sky_map

    if paired:
        half = chunk // 2
        main = jnp.transpose(power_spectrum[:, :, : depth // 2], (2, 0, 1)).reshape(
            count, half, local_x, local_y
        )
        middle = jnp.broadcast_to(
            power_spectrum[None, None, :, :, depth // 2], (count, 1, local_x, local_y)
        )
        power_blocks = jnp.concatenate([main, middle], axis=1)
        rows = half + 1
    else:
        power_blocks = jnp.transpose(power_spectrum, (2, 0, 1)).reshape(count, chunk, local_x, local_y)
        rows = chunk
    power_received = exchange(power_blocks)
    first = exchange(channel_blocks(noise_weight * right_side))
    power_planes = jnp.transpose(to_planes_of(power_received, rows), (2, 0, 3, 1, 4)).reshape(
        rows, full_x, full_y
    )
    if paired:
        device = lax.axis_index("wide") * n_narrow + lax.axis_index("narrow")
        second = jnp.where(device == 0, power_planes[half], power_planes[0])
        weights = jnp.concatenate(
            [power_planes[0:1], second[None], jnp.repeat(power_planes[1:half], 2, axis=0)], axis=0
        )
    else:
        weights = power_planes
    weights = weights * inverse_cells

    lanes = 32

    def lane_sums(left, right):
        return jnp.sum(jnp.sum(left * right, axis=(0, 1)).reshape(-1, lanes), axis=0)

    image_1 = right_side + noise_weight * finish(exchange(smoothed_spectral(first, weights)))
    sent = exchange(channel_blocks(noise_weight * image_1))
    returned = smoothed_spectral(sent, weights)
    cross = jnp.sum(sent * returned, axis=(0, 1, 2))
    cross = jnp.pad(cross, (0, lanes - cross.shape[0] % lanes if cross.shape[0] % lanes else 0))
    cross = jnp.sum(cross.reshape(-1, lanes), axis=0)
    image_norm = lane_sums(image_1, image_1)
    partials = jnp.stack(
        [lane_sums(right_side, right_side), lane_sums(right_side, image_1), image_norm, image_norm + cross]
    )
    block = chunk * local_x * local_y
    back = exchange(
        jnp.concatenate(
            [returned.reshape(count, block), jnp.broadcast_to(partials.reshape(1, 4 * lanes), (count, 4 * lanes))],
            axis=1,
        )
    )
    image_2 = image_1 + noise_weight * finish(back[:, :block].reshape(count, local_x, chunk, local_y))
    summed = jnp.sum(back[:, block:].reshape(count, 4, lanes), axis=0)
    totals = contract("vl,lm->vm", summed, jnp.ones((lanes, depth), jnp.float32))
    moments = totals.reshape(4, 1, 1, depth)
    norm_0, curvature_1, image_norm, cross = moments[0], moments[1], moments[2], moments[3]
    step_1 = norm_0 / curvature_1
    norm_1 = norm_0 - 2.0 * step_1 * curvature_1 + step_1 * step_1 * image_norm
    grow = 1.0 + norm_1 / norm_0
    curvature_2 = grow * grow * curvature_1 - 2.0 * step_1 * grow * image_norm + step_1 * step_1 * cross
    step_2 = norm_1 / curvature_2
    lead = step_1 + step_2 * grow
    tail = step_2 * step_1
    solution = lead * right_side - tail * image_1
    residual = right_side - lead * image_1 + tail * image_2
    return (solution, residual)


def solution(mesh):
    return jax.shard_map(
        local,
        mesh=mesh,
        in_specs=(P("wide", "narrow", None), P("wide", "narrow", None), P("wide", "narrow", None)),
        out_specs=(P("wide", "narrow", None), P("wide", "narrow", None)),
        check_vma=False,
    )
```

```python
import math

import jax
import jax.numpy as jnp
import numpy as np
from jax import lax
from jax.sharding import PartitionSpec as P

ITERS = 2

AXES = ("wide", "narrow")

highest = lax.Precision.HIGHEST


def cas_matrix(length, columns=None):
    counter = np.arange(length, dtype=np.int64)
    frequency = counter if columns is None else np.asarray(columns, np.int64)
    phase = counter[:, None] * frequency[None, :] % length
    angle = phase.astype(np.float64) * (2.0 * math.pi / length)
    return jnp.asarray((np.cos(angle) + np.sin(angle)).astype(np.float32))


def channel_order(depth, count):
    chunk = depth // count
    if chunk % 2:
        return list(range(depth)), False
    half = chunk // 2
    order = [0, depth // 2]
    for k in range(1, half):
        order += [k, depth - k]
    for k in range(half, depth // 2):
        order += [k, depth - k]
    return order, True


def contract(spec, values, matrix):
    return jnp.einsum(spec, values, matrix, precision=highest, preferred_element_type=jnp.float32)


def exchange(blocks):
    return lax.all_to_all(blocks, AXES, 0, 0, tiled=True)


def global_sums(partials):
    count = lax.axis_size("wide") * lax.axis_size("narrow")
    spread = jnp.broadcast_to(partials[None], (count,) + partials.shape)
    return jnp.sum(exchange(spread), axis=0)


def local(sky_map, noise_weight, power_spectrum):
    local_x, local_y, depth = sky_map.shape
    n_wide = lax.axis_size("wide")
    n_narrow = lax.axis_size("narrow")
    count = n_wide * n_narrow
    chunk = depth // count
    full_x = local_x * n_wide
    full_y = local_y * n_narrow
    matrix_x = cas_matrix(full_x).reshape(n_wide, local_x, full_x)
    matrix_y = cas_matrix(full_y).reshape(n_narrow, local_y, full_y)
    order, paired = channel_order(depth, count)
    matrix_z = cas_matrix(depth, order)
    inverse_cells = 1.0 / float(full_x * full_y * depth)

    def to_planes_of(blocks, rows):
        return blocks.reshape(n_wide, n_narrow, rows, local_x, local_y)

    def to_planes(blocks):
        return blocks.reshape(n_wide, n_narrow, local_x, chunk, local_y)

    def forward_sky(planes):
        along_y = contract("wnakb,nby->wkay", planes, matrix_y)
        return contract("wkay,wax->kxy", along_y, matrix_x)

    def inverse_sky(spectral):
        along_x = contract("kxy,wax->wkay", spectral, matrix_x)
        along_y = contract("wkay,nby->wnakb", along_x, matrix_y)
        return along_y.reshape(count, local_x, chunk, local_y)

    def channel_blocks(values):
        return contract("abz,zdk->dakb", values, matrix_z.reshape(depth, count, chunk))

    def finish(blocks):
        return contract("dakb,zdk->abz", blocks, matrix_z.reshape(depth, count, chunk))

    def smoothed_spectral(blocks, weights):
        return inverse_sky(forward_sky(to_planes(blocks)) * weights)

    right_side = noise_weight * sky_map

    if paired:
        half = chunk // 2
        power_blocks = jnp.transpose(power_spectrum[:, :, : depth // 2], (2, 0, 1)).reshape(
            count, half, local_x, local_y
        )
        rows = half
    else:
        power_blocks = jnp.transpose(power_spectrum, (2, 0, 1)).reshape(count, chunk, local_x, local_y)
        rows = chunk
    power_received = exchange(power_blocks)
    first = channel_blocks(noise_weight * right_side)
    if paired:
        middle = jnp.broadcast_to(
            power_spectrum[None, :, None, :, depth // 2], (count, local_x, 1, local_y)
        )
        first = exchange(jnp.concatenate([first, middle], axis=2))
        middle_plane = jnp.transpose(
            first[:, :, chunk:].reshape(n_wide, n_narrow, local_x, local_y), (0, 2, 1, 3)
        ).reshape(full_x, full_y)
        first = first[:, :, :chunk]
    else:
        first = exchange(first)
    power_planes = jnp.transpose(to_planes_of(power_received, rows), (2, 0, 3, 1, 4)).reshape(
        rows, full_x, full_y
    )
    if paired:
        device = lax.axis_index("wide") * n_narrow + lax.axis_index("narrow")
        second = jnp.where(device == 0, middle_plane, power_planes[0])
        weights = jnp.concatenate(
            [power_planes[0:1], second[None], jnp.repeat(power_planes[1:half], 2, axis=0)], axis=0
        )
    else:
        weights = power_planes
    weights = weights * inverse_cells

    lanes = 32

    def lane_sums(left, right):
        return jnp.sum(jnp.sum(left * right, axis=(0, 1)).reshape(-1, lanes), axis=0)

    image_1 = right_side + noise_weight * finish(exchange(smoothed_spectral(first, weights)))
    sent = exchange(channel_blocks(noise_weight * image_1))
    returned = smoothed_spectral(sent, weights)
    cross = jnp.sum(sent * returned, axis=(0, 1, 2))
    cross = jnp.pad(cross, (0, lanes - cross.shape[0] % lanes if cross.shape[0] % lanes else 0))
    cross = jnp.sum(cross.reshape(-1, lanes), axis=0)
    image_norm = lane_sums(image_1, image_1)
    partials = jnp.stack(
        [lane_sums(right_side, right_side), lane_sums(right_side, image_1), image_norm, image_norm + cross]
    )
    block = chunk * local_x * local_y
    back = exchange(
        jnp.concatenate(
            [jnp.broadcast_to(partials.reshape(1, 4 * lanes), (count, 4 * lanes)), returned.reshape(count, block)],
            axis=1,
        )
    )
    image_2 = image_1 + noise_weight * finish(back[:, 4 * lanes :].reshape(count, local_x, chunk, local_y))
    summed = jnp.sum(back[:, : 4 * lanes].reshape(count, 4, lanes), axis=0)
    totals = contract("vl,lm->vm", summed, jnp.ones((lanes, depth), jnp.float32))
    moments = totals.reshape(4, 1, 1, depth)
    norm_0, curvature_1, image_norm, cross = moments[0], moments[1], moments[2], moments[3]
    step_1 = norm_0 / curvature_1
    norm_1 = norm_0 - 2.0 * step_1 * curvature_1 + step_1 * step_1 * image_norm
    grow = 1.0 + norm_1 / norm_0
    curvature_2 = grow * grow * curvature_1 - 2.0 * step_1 * grow * image_norm + step_1 * step_1 * cross
    step_2 = norm_1 / curvature_2
    lead = step_1 + step_2 * grow
    tail = step_2 * step_1
    solution = lead * right_side - tail * image_1
    residual = right_side - lead * image_1 + tail * image_2
    return (solution, residual)


def solution(mesh):
    return jax.shard_map(
        local,
        mesh=mesh,
        in_specs=(P("wide", "narrow", None), P("wide", "narrow", None), P("wide", "narrow", None)),
        out_specs=(P("wide", "narrow", None), P("wide", "narrow", None)),
        check_vma=False,
    )
```

```python
import math

import jax
import jax.numpy as jnp
import numpy as np
from jax import lax
from jax.sharding import PartitionSpec as P

ITERS = 2

AXES = ("wide", "narrow")

highest = lax.Precision.HIGHEST


def cas_matrix(length, columns=None):
    counter = np.arange(length, dtype=np.int64)
    frequency = counter if columns is None else np.asarray(columns, np.int64)
    phase = counter[:, None] * frequency[None, :] % length
    angle = phase.astype(np.float64) * (2.0 * math.pi / length)
    return jnp.asarray((np.cos(angle) + np.sin(angle)).astype(np.float32))


def channel_order(depth, count):
    chunk = depth // count
    if chunk % 2:
        return list(range(depth)), False
    half = chunk // 2
    order = [0, depth // 2]
    for k in range(1, half):
        order += [k, depth - k]
    for k in range(half, depth // 2):
        order += [k, depth - k]
    return order, True


def contract(spec, values, matrix):
    return jnp.einsum(spec, values, matrix, precision=highest, preferred_element_type=jnp.float32)


def exchange(blocks):
    return lax.all_to_all(blocks, AXES, 0, 0, tiled=True)


def global_sums(partials):
    count = lax.axis_size("wide") * lax.axis_size("narrow")
    spread = jnp.broadcast_to(partials[None], (count,) + partials.shape)
    return jnp.sum(exchange(spread), axis=0)


def local(sky_map, noise_weight, power_spectrum):
    local_x, local_y, depth = sky_map.shape
    n_wide = lax.axis_size("wide")
    n_narrow = lax.axis_size("narrow")
    count = n_wide * n_narrow
    chunk = depth // count
    full_x = local_x * n_wide
    full_y = local_y * n_narrow
    matrix_x = cas_matrix(full_x).reshape(n_wide, local_x, full_x)
    matrix_y = cas_matrix(full_y).reshape(n_narrow, local_y, full_y)
    order, paired = channel_order(depth, count)
    matrix_z = cas_matrix(depth, order)
    inverse_cells = 1.0 / float(full_x * full_y * depth)

    def to_planes_of(blocks, rows):
        return blocks.reshape(n_wide, n_narrow, rows, local_x, local_y)

    def to_planes(blocks):
        return blocks.reshape(n_wide, n_narrow, local_x, chunk, local_y)

    def forward_sky(planes):
        along_y = contract("wnakb,nby->wkay", planes, matrix_y)
        return contract("wkay,wax->kxy", along_y, matrix_x)

    def inverse_sky(spectral):
        along_x = contract("kxy,wax->wkay", spectral, matrix_x)
        along_y = contract("wkay,nby->wnakb", along_x, matrix_y)
        return along_y.reshape(count, local_x, chunk, local_y)

    def channel_blocks(values):
        return contract("abz,zdk->dakb", values, matrix_z.reshape(depth, count, chunk))

    def finish(blocks):
        return contract("dakb,zdk->abz", blocks, matrix_z.reshape(depth, count, chunk))

    def smoothed_spectral(blocks, weights):
        return inverse_sky(forward_sky(to_planes(blocks)) * weights)

    right_side = noise_weight * sky_map

    if paired:
        half = chunk // 2
        main = jnp.transpose(power_spectrum[:, :, : depth // 2], (2, 0, 1)).reshape(
            count, half, local_x, local_y
        )
        middle = jnp.broadcast_to(
            power_spectrum[None, None, :, :, depth // 2], (count, 1, local_x, local_y)
        )
        power_blocks = jnp.concatenate([main, middle], axis=1)
        rows = half + 1
    else:
        power_blocks = jnp.transpose(power_spectrum, (2, 0, 1)).reshape(count, chunk, local_x, local_y)
        rows = chunk
    power_received = exchange(power_blocks)
    first = exchange(channel_blocks(noise_weight * right_side))
    power_planes = jnp.transpose(to_planes_of(power_received, rows), (2, 0, 3, 1, 4)).reshape(
        rows, full_x, full_y
    )
    if paired:
        device = lax.axis_index("wide") * n_narrow + lax.axis_index("narrow")
        second = jnp.where(device == 0, power_planes[half], power_planes[0])
        weights = jnp.concatenate(
            [power_planes[0:1], second[None], jnp.repeat(power_planes[1:half], 2, axis=0)], axis=0
        )
    else:
        weights = power_planes
    weights = weights * inverse_cells

    lanes = 32

    def lane_sums(left, right):
        return jnp.sum(jnp.sum(left * right, axis=(0, 1)).reshape(-1, lanes), axis=0)

    image_1 = right_side + noise_weight * finish(exchange(smoothed_spectral(first, weights)))
    sent = exchange(channel_blocks(noise_weight * image_1))
    spectrum = forward_sky(to_planes(sent))
    weighted = spectrum * weights
    returned = inverse_sky(weighted)
    cross = jnp.sum(spectrum * weighted, axis=(0, 1))
    cross = jnp.pad(cross, (0, lanes - cross.shape[0] % lanes if cross.shape[0] % lanes else 0))
    cross = jnp.sum(cross.reshape(-1, lanes), axis=0)
    image_norm = lane_sums(image_1, image_1)
    partials = jnp.stack(
        [lane_sums(right_side, right_side), lane_sums(right_side, image_1), image_norm, image_norm + cross]
    )
    block = chunk * local_x * local_y
    back = exchange(
        jnp.concatenate(
            [jnp.broadcast_to(partials.reshape(1, 4 * lanes), (count, 4 * lanes)), returned.reshape(count, block)],
            axis=1,
        )
    )
    image_2 = image_1 + noise_weight * finish(back[:, 4 * lanes :].reshape(count, local_x, chunk, local_y))
    summed = jnp.sum(back[:, : 4 * lanes].reshape(count, 4, lanes), axis=0)
    totals = contract("vl,lm->vm", summed, jnp.ones((lanes, depth), jnp.float32))
    moments = totals.reshape(4, 1, 1, depth)
    norm_0, curvature_1, image_norm, cross = moments[0], moments[1], moments[2], moments[3]
    step_1 = norm_0 / curvature_1
    norm_1 = norm_0 - 2.0 * step_1 * curvature_1 + step_1 * step_1 * image_norm
    grow = 1.0 + norm_1 / norm_0
    curvature_2 = grow * grow * curvature_1 - 2.0 * step_1 * grow * image_norm + step_1 * step_1 * cross
    step_2 = norm_1 / curvature_2
    lead = step_1 + step_2 * grow
    tail = step_2 * step_1
    solution = lead * right_side - tail * image_1
    residual = right_side - lead * image_1 + tail * image_2
    return (solution, residual)


def solution(mesh):
    return jax.shard_map(
        local,
        mesh=mesh,
        in_specs=(P("wide", "narrow", None), P("wide", "narrow", None), P("wide", "narrow", None)),
        out_specs=(P("wide", "narrow", None), P("wide", "narrow", None)),
        check_vma=False,
    )
```

```python
import math

import jax
import jax.numpy as jnp
import numpy as np
from jax import lax
from jax.sharding import PartitionSpec as P

ITERS = 2

AXES = ("wide", "narrow")

highest = lax.Precision.HIGHEST


def cas_matrix(length, columns=None):
    counter = np.arange(length, dtype=np.int64)
    frequency = counter if columns is None else np.asarray(columns, np.int64)
    phase = counter[:, None] * frequency[None, :] % length
    angle = phase.astype(np.float64) * (2.0 * math.pi / length)
    return jnp.asarray((np.cos(angle) + np.sin(angle)).astype(np.float32))


def channel_order(depth, count):
    chunk = depth // count
    if chunk % 2:
        return list(range(depth)), False
    half = chunk // 2
    order = [0, depth // 2]
    for k in range(1, half):
        order += [k, depth - k]
    for k in range(half, depth // 2):
        order += [k, depth - k]
    return order, True


def contract(spec, values, matrix):
    return jnp.einsum(spec, values, matrix, precision=highest, preferred_element_type=jnp.float32)


def exchange(blocks):
    return lax.all_to_all(blocks, AXES, 0, 0, tiled=True)


def global_sums(partials):
    count = lax.axis_size("wide") * lax.axis_size("narrow")
    spread = jnp.broadcast_to(partials[None], (count,) + partials.shape)
    return jnp.sum(exchange(spread), axis=0)


def local(sky_map, noise_weight, power_spectrum):
    local_x, local_y, depth = sky_map.shape
    n_wide = lax.axis_size("wide")
    n_narrow = lax.axis_size("narrow")
    count = n_wide * n_narrow
    chunk = depth // count
    full_x = local_x * n_wide
    full_y = local_y * n_narrow
    matrix_x = cas_matrix(full_x).reshape(n_wide, local_x, full_x)
    matrix_y = cas_matrix(full_y).reshape(n_narrow, local_y, full_y)
    order, paired = channel_order(depth, count)
    matrix_z = cas_matrix(depth, order)
    inverse_cells = 1.0 / float(full_x * full_y * depth)

    def to_planes_of(blocks, rows):
        return blocks.reshape(n_wide, n_narrow, rows, local_x, local_y)

    def to_planes(blocks):
        return blocks.reshape(n_wide, n_narrow, local_x, chunk, local_y)

    def forward_sky(planes):
        along_y = contract("wnakb,nby->wkay", planes, matrix_y)
        return contract("wkay,wax->kxy", along_y, matrix_x)

    def inverse_sky(spectral):
        along_y = contract("kxy,nby->nkxb", spectral, matrix_y)
        along_x = contract("nkxb,wax->wnakb", along_y, matrix_x)
        return along_x.reshape(count, local_x, chunk, local_y)

    def channel_blocks(values):
        return contract("abz,zdk->dakb", values, matrix_z.reshape(depth, count, chunk))

    def finish(blocks):
        return contract("dakb,zdk->abz", blocks, matrix_z.reshape(depth, count, chunk))

    def smoothed_spectral(blocks, weights):
        return inverse_sky(forward_sky(to_planes(blocks)) * weights)

    right_side = noise_weight * sky_map

    if paired:
        half = chunk // 2
        main = jnp.transpose(power_spectrum[:, :, : depth // 2], (2, 0, 1)).reshape(
            count, half, local_x, local_y
        )
        middle = jnp.broadcast_to(
            power_spectrum[None, None, :, :, depth // 2], (count, 1, local_x, local_y)
        )
        power_blocks = jnp.concatenate([main, middle], axis=1)
        rows = half + 1
    else:
        power_blocks = jnp.transpose(power_spectrum, (2, 0, 1)).reshape(count, chunk, local_x, local_y)
        rows = chunk
    power_received = exchange(power_blocks)
    first = exchange(channel_blocks(noise_weight * right_side))
    power_planes = jnp.transpose(to_planes_of(power_received, rows), (2, 0, 3, 1, 4)).reshape(
        rows, full_x, full_y
    )
    if paired:
        device = lax.axis_index("wide") * n_narrow + lax.axis_index("narrow")
        second = jnp.where(device == 0, power_planes[half], power_planes[0])
        weights = jnp.concatenate(
            [power_planes[0:1], second[None], jnp.repeat(power_planes[1:half], 2, axis=0)], axis=0
        )
    else:
        weights = power_planes
    weights = weights * inverse_cells

    lanes = 32

    def lane_sums(left, right):
        return jnp.sum(jnp.sum(left * right, axis=(0, 1)).reshape(-1, lanes), axis=0)

    image_1 = right_side + noise_weight * finish(exchange(smoothed_spectral(first, weights)))
    sent = exchange(channel_blocks(noise_weight * image_1))
    returned = smoothed_spectral(sent, weights)
    cross = jnp.sum(sent * returned, axis=(0, 1, 2))
    cross = jnp.pad(cross, (0, lanes - cross.shape[0] % lanes if cross.shape[0] % lanes else 0))
    cross = jnp.sum(cross.reshape(-1, lanes), axis=0)
    image_norm = lane_sums(image_1, image_1)
    partials = jnp.stack(
        [lane_sums(right_side, right_side), lane_sums(right_side, image_1), image_norm, image_norm + cross]
    )
    block = chunk * local_x * local_y
    back = exchange(
        jnp.concatenate(
            [jnp.broadcast_to(partials.reshape(1, 4 * lanes), (count, 4 * lanes)), returned.reshape(count, block)],
            axis=1,
        )
    )
    image_2 = image_1 + noise_weight * finish(back[:, 4 * lanes :].reshape(count, local_x, chunk, local_y))
    summed = jnp.sum(back[:, : 4 * lanes].reshape(count, 4, lanes), axis=0)
    totals = contract("vl,lm->vm", summed, jnp.ones((lanes, depth), jnp.float32))
    moments = totals.reshape(4, 1, 1, depth)
    norm_0, curvature_1, image_norm, cross = moments[0], moments[1], moments[2], moments[3]
    step_1 = norm_0 / curvature_1
    norm_1 = norm_0 - 2.0 * step_1 * curvature_1 + step_1 * step_1 * image_norm
    grow = 1.0 + norm_1 / norm_0
    curvature_2 = grow * grow * curvature_1 - 2.0 * step_1 * grow * image_norm + step_1 * step_1 * cross
    step_2 = norm_1 / curvature_2
    lead = step_1 + step_2 * grow
    tail = step_2 * step_1
    solution = lead * right_side - tail * image_1
    residual = right_side - lead * image_1 + tail * image_2
    return (solution, residual)


def solution(mesh):
    return jax.shard_map(
        local,
        mesh=mesh,
        in_specs=(P("wide", "narrow", None), P("wide", "narrow", None), P("wide", "narrow", None)),
        out_specs=(P("wide", "narrow", None), P("wide", "narrow", None)),
        check_vma=False,
    )
```

```python
import math

import jax
import jax.numpy as jnp
import numpy as np
from jax import lax
from jax.sharding import PartitionSpec as P

ITERS = 2

AXES = ("wide", "narrow")

highest = lax.Precision.HIGHEST


def cas_matrix(length, columns=None):
    counter = np.arange(length, dtype=np.int64)
    frequency = counter if columns is None else np.asarray(columns, np.int64)
    phase = counter[:, None] * frequency[None, :] % length
    angle = phase.astype(np.float64) * (2.0 * math.pi / length)
    return jnp.asarray((np.cos(angle) + np.sin(angle)).astype(np.float32))


def channel_order(depth, count):
    chunk = depth // count
    if chunk % 2:
        return list(range(depth)), False
    half = chunk // 2
    order = [0, depth // 2]
    for k in range(1, half):
        order += [k, depth - k]
    for k in range(half, depth // 2):
        order += [k, depth - k]
    return order, True


def contract(spec, values, matrix):
    return jnp.einsum(spec, values, matrix, precision=highest, preferred_element_type=jnp.float32)


def exchange(blocks):
    return lax.all_to_all(blocks, AXES, 0, 0, tiled=True)


def global_sums(partials):
    count = lax.axis_size("wide") * lax.axis_size("narrow")
    spread = jnp.broadcast_to(partials[None], (count,) + partials.shape)
    return jnp.sum(exchange(spread), axis=0)


def local(sky_map, noise_weight, power_spectrum):
    local_x, local_y, depth = sky_map.shape
    n_wide = lax.axis_size("wide")
    n_narrow = lax.axis_size("narrow")
    count = n_wide * n_narrow
    chunk = depth // count
    full_x = local_x * n_wide
    full_y = local_y * n_narrow
    matrix_x = cas_matrix(full_x).reshape(n_wide, local_x, full_x)
    matrix_y = cas_matrix(full_y).reshape(n_narrow, local_y, full_y)
    order, paired = channel_order(depth, count)
    matrix_z = cas_matrix(depth, order)
    inverse_cells = 1.0 / float(full_x * full_y * depth)

    def to_planes_of(blocks, rows):
        return blocks.reshape(n_wide, n_narrow, rows, local_x, local_y)

    def to_planes(blocks):
        return blocks.reshape(n_wide, n_narrow, local_x, chunk, local_y)

    def forward_sky(planes):
        along_y = contract("wnakb,nby->wkay", planes, matrix_y)
        return contract("wkay,wax->xky", along_y, matrix_x)

    def inverse_sky(spectral):
        along_x = contract("xky,wax->wkay", spectral, matrix_x)
        along_y = contract("wkay,nby->wnakb", along_x, matrix_y)
        return along_y.reshape(count, local_x, chunk, local_y)

    def channel_blocks(values):
        return contract("abz,zdk->dakb", values, matrix_z.reshape(depth, count, chunk))

    def finish(blocks):
        return contract("dakb,zdk->abz", blocks, matrix_z.reshape(depth, count, chunk))

    def smoothed_spectral(blocks, weights):
        return inverse_sky(forward_sky(to_planes(blocks)) * weights)

    right_side = noise_weight * sky_map

    if paired:
        half = chunk // 2
        main = jnp.transpose(power_spectrum[:, :, : depth // 2], (2, 0, 1)).reshape(
            count, half, local_x, local_y
        )
        middle = jnp.broadcast_to(
            power_spectrum[None, None, :, :, depth // 2], (count, 1, local_x, local_y)
        )
        power_blocks = jnp.concatenate([main, middle], axis=1)
        rows = half + 1
    else:
        power_blocks = jnp.transpose(power_spectrum, (2, 0, 1)).reshape(count, chunk, local_x, local_y)
        rows = chunk
    power_received = exchange(power_blocks)
    first = exchange(channel_blocks(noise_weight * right_side))
    power_planes = jnp.transpose(to_planes_of(power_received, rows), (2, 0, 3, 1, 4)).reshape(
        rows, full_x, full_y
    )
    if paired:
        device = lax.axis_index("wide") * n_narrow + lax.axis_index("narrow")
        second = jnp.where(device == 0, power_planes[half], power_planes[0])
        weights = jnp.concatenate(
            [power_planes[0:1], second[None], jnp.repeat(power_planes[1:half], 2, axis=0)], axis=0
        )
    else:
        weights = power_planes
    weights = jnp.transpose(weights, (1, 0, 2)) * inverse_cells

    lanes = 32

    def lane_sums(left, right):
        return jnp.sum(jnp.sum(left * right, axis=(0, 1)).reshape(-1, lanes), axis=0)

    image_1 = right_side + noise_weight * finish(exchange(smoothed_spectral(first, weights)))
    sent = exchange(channel_blocks(noise_weight * image_1))
    returned = smoothed_spectral(sent, weights)
    cross = jnp.sum(sent * returned, axis=(0, 1, 2))
    cross = jnp.pad(cross, (0, lanes - cross.shape[0] % lanes if cross.shape[0] % lanes else 0))
    cross = jnp.sum(cross.reshape(-1, lanes), axis=0)
    image_norm = lane_sums(image_1, image_1)
    partials = jnp.stack(
        [lane_sums(right_side, right_side), lane_sums(right_side, image_1), image_norm, image_norm + cross]
    )
    block = chunk * local_x * local_y
    back = exchange(
        jnp.concatenate(
            [jnp.broadcast_to(partials.reshape(1, 4 * lanes), (count, 4 * lanes)), returned.reshape(count, block)],
            axis=1,
        )
    )
    image_2 = image_1 + noise_weight * finish(back[:, 4 * lanes :].reshape(count, local_x, chunk, local_y))
    summed = jnp.sum(back[:, : 4 * lanes].reshape(count, 4, lanes), axis=0)
    totals = contract("vl,lm->vm", summed, jnp.ones((lanes, depth), jnp.float32))
    moments = totals.reshape(4, 1, 1, depth)
    norm_0, curvature_1, image_norm, cross = moments[0], moments[1], moments[2], moments[3]
    step_1 = norm_0 / curvature_1
    norm_1 = norm_0 - 2.0 * step_1 * curvature_1 + step_1 * step_1 * image_norm
    grow = 1.0 + norm_1 / norm_0
    curvature_2 = grow * grow * curvature_1 - 2.0 * step_1 * grow * image_norm + step_1 * step_1 * cross
    step_2 = norm_1 / curvature_2
    lead = step_1 + step_2 * grow
    tail = step_2 * step_1
    solution = lead * right_side - tail * image_1
    residual = right_side - lead * image_1 + tail * image_2
    return (solution, residual)


def solution(mesh):
    return jax.shard_map(
        local,
        mesh=mesh,
        in_specs=(P("wide", "narrow", None), P("wide", "narrow", None), P("wide", "narrow", None)),
        out_specs=(P("wide", "narrow", None), P("wide", "narrow", None)),
        check_vma=False,
    )
```

```python
import math

import jax
import jax.numpy as jnp
import numpy as np
from jax import lax
from jax.sharding import PartitionSpec as P

ITERS = 2

AXES = ("wide", "narrow")

highest = lax.Precision.HIGHEST


def cas_matrix(length, columns=None):
    counter = np.arange(length, dtype=np.int64)
    frequency = counter if columns is None else np.asarray(columns, np.int64)
    phase = counter[:, None] * frequency[None, :] % length
    angle = phase.astype(np.float64) * (2.0 * math.pi / length)
    return jnp.asarray((np.cos(angle) + np.sin(angle)).astype(np.float32))


def channel_order(depth, count):
    chunk = depth // count
    if chunk % 2:
        return list(range(depth)), False
    half = chunk // 2
    order = [0, depth // 2]
    for k in range(1, half):
        order += [k, depth - k]
    for k in range(half, depth // 2):
        order += [k, depth - k]
    return order, True


def contract(spec, values, matrix):
    return jnp.einsum(spec, values, matrix, precision=highest, preferred_element_type=jnp.float32)


def exchange(blocks):
    return lax.all_to_all(blocks, AXES, 0, 0, tiled=True)


def global_sums(partials):
    count = lax.axis_size("wide") * lax.axis_size("narrow")
    spread = jnp.broadcast_to(partials[None], (count,) + partials.shape)
    return jnp.sum(exchange(spread), axis=0)


def local(sky_map, noise_weight, power_spectrum):
    local_x, local_y, depth = sky_map.shape
    n_wide = lax.axis_size("wide")
    n_narrow = lax.axis_size("narrow")
    count = n_wide * n_narrow
    chunk = depth // count
    full_x = local_x * n_wide
    full_y = local_y * n_narrow
    matrix_x = cas_matrix(full_x).reshape(n_wide, local_x, full_x)
    matrix_y = cas_matrix(full_y).reshape(n_narrow, local_y, full_y)
    order, paired = channel_order(depth, count)
    matrix_z = cas_matrix(depth, order)
    inverse_cells = 1.0 / float(full_x * full_y * depth)

    def to_planes_of(blocks, rows):
        return blocks.reshape(n_wide, n_narrow, rows, local_x, local_y)

    def to_planes(blocks):
        return blocks.reshape(n_wide, n_narrow, local_x, chunk, local_y)

    def forward_sky(planes):
        along_y = contract("wnakb,nby->waky", planes, matrix_y)
        return contract("waky,wax->xky", along_y, matrix_x)

    def inverse_sky(spectral):
        along_x = contract("xky,wax->waky", spectral, matrix_x)
        along_y = contract("waky,nby->wnakb", along_x, matrix_y)
        return along_y.reshape(count, local_x, chunk, local_y)

    def channel_blocks(values):
        return contract("abz,zdk->dakb", values, matrix_z.reshape(depth, count, chunk))

    def finish(blocks):
        return contract("dakb,zdk->abz", blocks, matrix_z.reshape(depth, count, chunk))

    def smoothed_spectral(blocks, weights):
        return inverse_sky(forward_sky(to_planes(blocks)) * weights)

    right_side = noise_weight * sky_map

    if paired:
        half = chunk // 2
        main = jnp.transpose(power_spectrum[:, :, : depth // 2], (2, 0, 1)).reshape(
            count, half, local_x, local_y
        )
        middle = jnp.broadcast_to(
            power_spectrum[None, None, :, :, depth // 2], (count, 1, local_x, local_y)
        )
        power_blocks = jnp.concatenate([main, middle], axis=1)
        rows = half + 1
    else:
        power_blocks = jnp.transpose(power_spectrum, (2, 0, 1)).reshape(count, chunk, local_x, local_y)
        rows = chunk
    power_received = exchange(power_blocks)
    first = exchange(channel_blocks(noise_weight * right_side))
    power_planes = jnp.transpose(to_planes_of(power_received, rows), (2, 0, 3, 1, 4)).reshape(
        rows, full_x, full_y
    )
    if paired:
        device = lax.axis_index("wide") * n_narrow + lax.axis_index("narrow")
        second = jnp.where(device == 0, power_planes[half], power_planes[0])
        weights = jnp.concatenate(
            [power_planes[0:1], second[None], jnp.repeat(power_planes[1:half], 2, axis=0)], axis=0
        )
    else:
        weights = power_planes
    weights = jnp.transpose(weights, (1, 0, 2)) * inverse_cells

    lanes = 32

    def lane_sums(left, right):
        return jnp.sum(jnp.sum(left * right, axis=(0, 1)).reshape(-1, lanes), axis=0)

    image_1 = right_side + noise_weight * finish(exchange(smoothed_spectral(first, weights)))
    sent = exchange(channel_blocks(noise_weight * image_1))
    returned = smoothed_spectral(sent, weights)
    cross = jnp.sum(sent * returned, axis=(0, 1, 2))
    cross = jnp.pad(cross, (0, lanes - cross.shape[0] % lanes if cross.shape[0] % lanes else 0))
    cross = jnp.sum(cross.reshape(-1, lanes), axis=0)
    image_norm = lane_sums(image_1, image_1)
    partials = jnp.stack(
        [lane_sums(right_side, right_side), lane_sums(right_side, image_1), image_norm, image_norm + cross]
    )
    block = chunk * local_x * local_y
    back = exchange(
        jnp.concatenate(
            [jnp.broadcast_to(partials.reshape(1, 4 * lanes), (count, 4 * lanes)), returned.reshape(count, block)],
            axis=1,
        )
    )
    image_2 = image_1 + noise_weight * finish(back[:, 4 * lanes :].reshape(count, local_x, chunk, local_y))
    summed = jnp.sum(back[:, : 4 * lanes].reshape(count, 4, lanes), axis=0)
    totals = contract("vl,lm->vm", summed, jnp.ones((lanes, depth), jnp.float32))
    moments = totals.reshape(4, 1, 1, depth)
    norm_0, curvature_1, image_norm, cross = moments[0], moments[1], moments[2], moments[3]
    step_1 = norm_0 / curvature_1
    norm_1 = norm_0 - 2.0 * step_1 * curvature_1 + step_1 * step_1 * image_norm
    grow = 1.0 + norm_1 / norm_0
    curvature_2 = grow * grow * curvature_1 - 2.0 * step_1 * grow * image_norm + step_1 * step_1 * cross
    step_2 = norm_1 / curvature_2
    lead = step_1 + step_2 * grow
    tail = step_2 * step_1
    solution = lead * right_side - tail * image_1
    residual = right_side - lead * image_1 + tail * image_2
    return (solution, residual)


def solution(mesh):
    return jax.shard_map(
        local,
        mesh=mesh,
        in_specs=(P("wide", "narrow", None), P("wide", "narrow", None), P("wide", "narrow", None)),
        out_specs=(P("wide", "narrow", None), P("wide", "narrow", None)),
        check_vma=False,
    )
```

```python
import math

import jax
import jax.numpy as jnp
import numpy as np
from jax import lax
from jax.sharding import PartitionSpec as P

ITERS = 2

AXES = ("wide", "narrow")

highest = lax.Precision.HIGHEST


def cas_matrix(length, columns=None):
    counter = np.arange(length, dtype=np.int64)
    frequency = counter if columns is None else np.asarray(columns, np.int64)
    phase = counter[:, None] * frequency[None, :] % length
    angle = phase.astype(np.float64) * (2.0 * math.pi / length)
    return jnp.asarray((np.cos(angle) + np.sin(angle)).astype(np.float32))


def channel_order(depth, count):
    chunk = depth // count
    if chunk % 2:
        return list(range(depth)), False
    half = chunk // 2
    order = [0, depth // 2]
    for k in range(1, half):
        order += [k, depth - k]
    for k in range(half, depth // 2):
        order += [k, depth - k]
    return order, True


def contract(spec, values, matrix):
    return jnp.einsum(spec, values, matrix, precision=highest, preferred_element_type=jnp.float32)


def exchange(blocks):
    return lax.all_to_all(blocks, AXES, 0, 0, tiled=True)


def global_sums(partials):
    count = lax.axis_size("wide") * lax.axis_size("narrow")
    spread = jnp.broadcast_to(partials[None], (count,) + partials.shape)
    return jnp.sum(exchange(spread), axis=0)


def local(sky_map, noise_weight, power_spectrum):
    local_x, local_y, depth = sky_map.shape
    n_wide = lax.axis_size("wide")
    n_narrow = lax.axis_size("narrow")
    count = n_wide * n_narrow
    chunk = depth // count
    full_x = local_x * n_wide
    full_y = local_y * n_narrow
    matrix_x = cas_matrix(full_x).reshape(n_wide, local_x, full_x)
    matrix_y = cas_matrix(full_y).reshape(n_narrow, local_y, full_y)
    order, paired = channel_order(depth, count)
    matrix_z = cas_matrix(depth, order)
    inverse_cells = 1.0 / float(full_x * full_y * depth)

    def to_planes_of(blocks, rows):
        return blocks.reshape(n_wide, n_narrow, rows, local_x, local_y)

    def to_planes(blocks):
        return blocks.reshape(n_wide, n_narrow, local_x, chunk, local_y)

    def forward_sky(planes):
        along_y = contract("wnakb,nby->kway", planes, matrix_y)
        return contract("kway,wax->xky", along_y, matrix_x)

    def inverse_sky(spectral):
        along_x = contract("xky,wax->kway", spectral, matrix_x)
        along_y = contract("kway,nby->wnakb", along_x, matrix_y)
        return along_y.reshape(count, local_x, chunk, local_y)

    def channel_blocks(values):
        return contract("abz,zdk->dakb", values, matrix_z.reshape(depth, count, chunk))

    def finish(blocks):
        return contract("dakb,zdk->abz", blocks, matrix_z.reshape(depth, count, chunk))

    def smoothed_spectral(blocks, weights):
        return inverse_sky(forward_sky(to_planes(blocks)) * weights)

    right_side = noise_weight * sky_map

    if paired:
        half = chunk // 2
        main = jnp.transpose(power_spectrum[:, :, : depth // 2], (2, 0, 1)).reshape(
            count, half, local_x, local_y
        )
        middle = jnp.broadcast_to(
            power_spectrum[None, None, :, :, depth // 2], (count, 1, local_x, local_y)
        )
        power_blocks = jnp.concatenate([main, middle], axis=1)
        rows = half + 1
    else:
        power_blocks = jnp.transpose(power_spectrum, (2, 0, 1)).reshape(count, chunk, local_x, local_y)
        rows = chunk
    power_received = exchange(power_blocks)
    first = exchange(channel_blocks(noise_weight * right_side))
    power_planes = jnp.transpose(to_planes_of(power_received, rows), (2, 0, 3, 1, 4)).reshape(
        rows, full_x, full_y
    )
    if paired:
        device = lax.axis_index("wide") * n_narrow + lax.axis_index("narrow")
        second = jnp.where(device == 0, power_planes[half], power_planes[0])
        weights = jnp.concatenate(
            [power_planes[0:1], second[None], jnp.repeat(power_planes[1:half], 2, axis=0)], axis=0
        )
    else:
        weights = power_planes
    weights = jnp.transpose(weights, (1, 0, 2)) * inverse_cells

    lanes = 32

    def lane_sums(left, right):
        return jnp.sum(jnp.sum(left * right, axis=(0, 1)).reshape(-1, lanes), axis=0)

    image_1 = right_side + noise_weight * finish(exchange(smoothed_spectral(first, weights)))
    sent = exchange(channel_blocks(noise_weight * image_1))
    returned = smoothed_spectral(sent, weights)
    cross = jnp.sum(sent * returned, axis=(0, 1, 2))
    cross = jnp.pad(cross, (0, lanes - cross.shape[0] % lanes if cross.shape[0] % lanes else 0))
    cross = jnp.sum(cross.reshape(-1, lanes), axis=0)
    image_norm = lane_sums(image_1, image_1)
    partials = jnp.stack(
        [lane_sums(right_side, right_side), lane_sums(right_side, image_1), image_norm, image_norm + cross]
    )
    block = chunk * local_x * local_y
    back = exchange(
        jnp.concatenate(
            [jnp.broadcast_to(partials.reshape(1, 4 * lanes), (count, 4 * lanes)), returned.reshape(count, block)],
            axis=1,
        )
    )
    image_2 = image_1 + noise_weight * finish(back[:, 4 * lanes :].reshape(count, local_x, chunk, local_y))
    summed = jnp.sum(back[:, : 4 * lanes].reshape(count, 4, lanes), axis=0)
    totals = contract("vl,lm->vm", summed, jnp.ones((lanes, depth), jnp.float32))
    moments = totals.reshape(4, 1, 1, depth)
    norm_0, curvature_1, image_norm, cross = moments[0], moments[1], moments[2], moments[3]
    step_1 = norm_0 / curvature_1
    norm_1 = norm_0 - 2.0 * step_1 * curvature_1 + step_1 * step_1 * image_norm
    grow = 1.0 + norm_1 / norm_0
    curvature_2 = grow * grow * curvature_1 - 2.0 * step_1 * grow * image_norm + step_1 * step_1 * cross
    step_2 = norm_1 / curvature_2
    lead = step_1 + step_2 * grow
    tail = step_2 * step_1
    solution = lead * right_side - tail * image_1
    residual = right_side - lead * image_1 + tail * image_2
    return (solution, residual)


def solution(mesh):
    return jax.shard_map(
        local,
        mesh=mesh,
        in_specs=(P("wide", "narrow", None), P("wide", "narrow", None), P("wide", "narrow", None)),
        out_specs=(P("wide", "narrow", None), P("wide", "narrow", None)),
        check_vma=False,
    )
```

```python
import math

import jax
import jax.numpy as jnp
import numpy as np
from jax import lax
from jax.sharding import PartitionSpec as P

ITERS = 2

AXES = ("wide", "narrow")

highest = lax.Precision.HIGHEST


def cas_matrix(length, columns=None):
    counter = np.arange(length, dtype=np.int64)
    frequency = counter if columns is None else np.asarray(columns, np.int64)
    phase = counter[:, None] * frequency[None, :] % length
    angle = phase.astype(np.float64) * (2.0 * math.pi / length)
    return jnp.asarray((np.cos(angle) + np.sin(angle)).astype(np.float32))


def channel_order(depth, count):
    chunk = depth // count
    if chunk % 2:
        return list(range(depth)), False
    half = chunk // 2
    order = [0, depth // 2]
    for k in range(1, half):
        order += [k, depth - k]
    for k in range(half, depth // 2):
        order += [k, depth - k]
    return order, True


def contract(spec, values, matrix):
    return jnp.einsum(spec, values, matrix, precision=highest, preferred_element_type=jnp.float32)


def exchange(blocks):
    return lax.all_to_all(blocks, AXES, 0, 0, tiled=True)


def global_sums(partials):
    count = lax.axis_size("wide") * lax.axis_size("narrow")
    spread = jnp.broadcast_to(partials[None], (count,) + partials.shape)
    return jnp.sum(exchange(spread), axis=0)


def local(sky_map, noise_weight, power_spectrum):
    local_x, local_y, depth = sky_map.shape
    n_wide = lax.axis_size("wide")
    n_narrow = lax.axis_size("narrow")
    count = n_wide * n_narrow
    chunk = depth // count
    full_x = local_x * n_wide
    full_y = local_y * n_narrow
    matrix_x = cas_matrix(full_x).reshape(n_wide, local_x, full_x)
    matrix_y = cas_matrix(full_y).reshape(n_narrow, local_y, full_y)
    order, paired = channel_order(depth, count)
    matrix_z = cas_matrix(depth, order)
    inverse_cells = 1.0 / float(full_x * full_y * depth)

    def to_planes_of(blocks, rows):
        return blocks.reshape(n_wide, n_narrow, rows, local_x, local_y)

    def to_planes(blocks):
        return blocks.reshape(n_wide, n_narrow, local_x, chunk, local_y)

    def forward_sky(planes):
        along_y = contract("wnakb,nby->kway", planes, matrix_y)
        return contract("kway,wax->kxy", along_y, matrix_x)

    def inverse_sky(spectral):
        along_x = contract("kxy,wax->kway", spectral, matrix_x)
        along_y = contract("kway,nby->wnakb", along_x, matrix_y)
        return along_y.reshape(count, local_x, chunk, local_y)

    def channel_blocks(values):
        return contract("abz,zdk->dakb", values, matrix_z.reshape(depth, count, chunk))

    def finish(blocks):
        return contract("dakb,zdk->abz", blocks, matrix_z.reshape(depth, count, chunk))

    def smoothed_spectral(blocks, weights):
        return inverse_sky(forward_sky(to_planes(blocks)) * weights)

    right_side = noise_weight * sky_map

    if paired:
        half = chunk // 2
        main = jnp.transpose(power_spectrum[:, :, : depth // 2], (2, 0, 1)).reshape(
            count, half, local_x, local_y
        )
        middle = jnp.broadcast_to(
            power_spectrum[None, None, :, :, depth // 2], (count, 1, local_x, local_y)
        )
        power_blocks = jnp.concatenate([main, middle], axis=1)
        rows = half + 1
    else:
        power_blocks = jnp.transpose(power_spectrum, (2, 0, 1)).reshape(count, chunk, local_x, local_y)
        rows = chunk
    power_received = exchange(power_blocks)
    first = exchange(channel_blocks(noise_weight * right_side))
    power_planes = jnp.transpose(to_planes_of(power_received, rows), (2, 0, 3, 1, 4)).reshape(
        rows, full_x, full_y
    )
    if paired:
        device = lax.axis_index("wide") * n_narrow + lax.axis_index("narrow")
        second = jnp.where(device == 0, power_planes[half], power_planes[0])
        weights = jnp.concatenate(
            [power_planes[0:1], second[None], jnp.repeat(power_planes[1:half], 2, axis=0)], axis=0
        )
    else:
        weights = power_planes
    weights = weights * inverse_cells

    lanes = 32

    def lane_sums(left, right):
        return jnp.sum(jnp.sum(left * right, axis=(0, 1)).reshape(-1, lanes), axis=0)

    image_1 = right_side + noise_weight * finish(exchange(smoothed_spectral(first, weights)))
    sent = exchange(channel_blocks(noise_weight * image_1))
    returned = smoothed_spectral(sent, weights)
    cross = jnp.sum(sent * returned, axis=(0, 1, 2))
    cross = jnp.pad(cross, (0, lanes - cross.shape[0] % lanes if cross.shape[0] % lanes else 0))
    cross = jnp.sum(cross.reshape(-1, lanes), axis=0)
    image_norm = lane_sums(image_1, image_1)
    partials = jnp.stack(
        [lane_sums(right_side, right_side), lane_sums(right_side, image_1), image_norm, image_norm + cross]
    )
    block = chunk * local_x * local_y
    back = exchange(
        jnp.concatenate(
            [jnp.broadcast_to(partials.reshape(1, 4 * lanes), (count, 4 * lanes)), returned.reshape(count, block)],
            axis=1,
        )
    )
    image_2 = image_1 + noise_weight * finish(back[:, 4 * lanes :].reshape(count, local_x, chunk, local_y))
    summed = jnp.sum(back[:, : 4 * lanes].reshape(count, 4, lanes), axis=0)
    totals = contract("vl,lm->vm", summed, jnp.ones((lanes, depth), jnp.float32))
    moments = totals.reshape(4, 1, 1, depth)
    norm_0, curvature_1, image_norm, cross = moments[0], moments[1], moments[2], moments[3]
    step_1 = norm_0 / curvature_1
    norm_1 = norm_0 - 2.0 * step_1 * curvature_1 + step_1 * step_1 * image_norm
    grow = 1.0 + norm_1 / norm_0
    curvature_2 = grow * grow * curvature_1 - 2.0 * step_1 * grow * image_norm + step_1 * step_1 * cross
    step_2 = norm_1 / curvature_2
    lead = step_1 + step_2 * grow
    tail = step_2 * step_1
    solution = lead * right_side - tail * image_1
    residual = right_side - lead * image_1 + tail * image_2
    return (solution, residual)


def solution(mesh):
    return jax.shard_map(
        local,
        mesh=mesh,
        in_specs=(P("wide", "narrow", None), P("wide", "narrow", None), P("wide", "narrow", None)),
        out_specs=(P("wide", "narrow", None), P("wide", "narrow", None)),
        check_vma=False,
    )
```

```python
import math

import jax
import jax.numpy as jnp
import numpy as np
from jax import lax
from jax.sharding import PartitionSpec as P

ITERS = 2

AXES = ("wide", "narrow")

highest = lax.Precision.HIGHEST


def cas_matrix(length, columns=None):
    counter = np.arange(length, dtype=np.int64)
    frequency = counter if columns is None else np.asarray(columns, np.int64)
    phase = counter[:, None] * frequency[None, :] % length
    angle = phase.astype(np.float64) * (2.0 * math.pi / length)
    return jnp.asarray((np.cos(angle) + np.sin(angle)).astype(np.float32))


def channel_order(depth, count):
    chunk = depth // count
    if chunk % 2:
        return list(range(depth)), False
    half = chunk // 2
    order = [0, depth // 2]
    for k in range(1, half):
        order += [k, depth - k]
    for k in range(half, depth // 2):
        order += [k, depth - k]
    return order, True


def contract(spec, values, matrix):
    return jnp.einsum(spec, values, matrix, precision=highest, preferred_element_type=jnp.float32)


def exchange(blocks):
    return lax.all_to_all(blocks, AXES, 0, 0, tiled=True)


def global_sums(partials):
    count = lax.axis_size("wide") * lax.axis_size("narrow")
    spread = jnp.broadcast_to(partials[None], (count,) + partials.shape)
    return jnp.sum(exchange(spread), axis=0)


def local(sky_map, noise_weight, power_spectrum):
    local_x, local_y, depth = sky_map.shape
    n_wide = lax.axis_size("wide")
    n_narrow = lax.axis_size("narrow")
    count = n_wide * n_narrow
    chunk = depth // count
    full_x = local_x * n_wide
    full_y = local_y * n_narrow
    matrix_x = cas_matrix(full_x).reshape(n_wide, local_x, full_x)
    matrix_y = cas_matrix(full_y).reshape(n_narrow, local_y, full_y)
    order, paired = channel_order(depth, count)
    matrix_z = cas_matrix(depth, order)
    inverse_cells = 1.0 / float(full_x * full_y * depth)

    def to_planes_of(blocks, rows):
        return blocks.reshape(n_wide, n_narrow, rows, local_x, local_y)

    def to_planes(blocks):
        return blocks.reshape(n_wide, n_narrow, local_x, chunk, local_y)

    def forward_sky(planes):
        along_y = contract("wnakb,nby->kway", planes, matrix_y)
        return contract("kway,wax->xky", along_y, matrix_x)

    def inverse_sky(spectral):
        along_x = contract("xky,wax->kway", spectral, matrix_x)
        along_y = contract("kway,nby->wnakb", along_x, matrix_y)
        return along_y.reshape(count, local_x, chunk, local_y)

    def channel_blocks(values):
        return contract("abz,zdk->dakb", values, matrix_z.reshape(depth, count, chunk))

    def finish(blocks):
        return contract("dakb,zdk->abz", blocks, matrix_z.reshape(depth, count, chunk))

    def smoothed_spectral(blocks, weights):
        return inverse_sky(forward_sky(to_planes(blocks)) * weights)

    right_side = noise_weight * sky_map
    lanes = 32

    def lane_sums(left, right):
        return jnp.sum(jnp.sum(left * right, axis=(0, 1)).reshape(-1, lanes), axis=0)

    if paired:
        half = chunk // 2
        main = jnp.transpose(power_spectrum[:, :, : depth // 2], (2, 0, 1)).reshape(
            count, half, local_x, local_y
        )
        middle = jnp.broadcast_to(
            power_spectrum[None, None, :, :, depth // 2], (count, 1, local_x, local_y)
        )
        power_blocks = jnp.concatenate([main, middle], axis=1)
        rows = half + 1
    else:
        power_blocks = jnp.transpose(power_spectrum, (2, 0, 1)).reshape(count, chunk, local_x, local_y)
        rows = chunk
    power_received = exchange(power_blocks)
    first_blocks, norm_lanes = lax.optimization_barrier(
        (channel_blocks(noise_weight * right_side), lane_sums(right_side, right_side))
    )
    first = exchange(first_blocks)
    power_planes = jnp.transpose(to_planes_of(power_received, rows), (2, 0, 3, 1, 4)).reshape(
        rows, full_x, full_y
    )
    if paired:
        device = lax.axis_index("wide") * n_narrow + lax.axis_index("narrow")
        second = jnp.where(device == 0, power_planes[half], power_planes[0])
        weights = jnp.concatenate(
            [power_planes[0:1], second[None], jnp.repeat(power_planes[1:half], 2, axis=0)], axis=0
        )
    else:
        weights = power_planes
    weights = jnp.transpose(weights, (1, 0, 2)) * inverse_cells

    image_1 = right_side + noise_weight * finish(exchange(smoothed_spectral(first, weights)))
    sent = exchange(channel_blocks(noise_weight * image_1))
    returned = smoothed_spectral(sent, weights)
    cross = jnp.sum(sent * returned, axis=(0, 1, 2))
    cross = jnp.pad(cross, (0, lanes - cross.shape[0] % lanes if cross.shape[0] % lanes else 0))
    cross = jnp.sum(cross.reshape(-1, lanes), axis=0)
    image_norm = lane_sums(image_1, image_1)
    partials = jnp.stack(
        [norm_lanes, lane_sums(right_side, image_1), image_norm, image_norm + cross]
    )
    block = chunk * local_x * local_y
    back = exchange(
        jnp.concatenate(
            [jnp.broadcast_to(partials.reshape(1, 4 * lanes), (count, 4 * lanes)), returned.reshape(count, block)],
            axis=1,
        )
    )
    image_2 = image_1 + noise_weight * finish(back[:, 4 * lanes :].reshape(count, local_x, chunk, local_y))
    summed = jnp.sum(back[:, : 4 * lanes].reshape(count, 4, lanes), axis=0)
    totals = contract("vl,lm->vm", summed, jnp.ones((lanes, depth), jnp.float32))
    moments = totals.reshape(4, 1, 1, depth)
    norm_0, curvature_1, image_norm, cross = moments[0], moments[1], moments[2], moments[3]
    step_1 = norm_0 / curvature_1
    norm_1 = norm_0 - 2.0 * step_1 * curvature_1 + step_1 * step_1 * image_norm
    grow = 1.0 + norm_1 / norm_0
    curvature_2 = grow * grow * curvature_1 - 2.0 * step_1 * grow * image_norm + step_1 * step_1 * cross
    step_2 = norm_1 / curvature_2
    lead = step_1 + step_2 * grow
    tail = step_2 * step_1
    solution = lead * right_side - tail * image_1
    residual = right_side - lead * image_1 + tail * image_2
    return (solution, residual)


def solution(mesh):
    return jax.shard_map(
        local,
        mesh=mesh,
        in_specs=(P("wide", "narrow", None), P("wide", "narrow", None), P("wide", "narrow", None)),
        out_specs=(P("wide", "narrow", None), P("wide", "narrow", None)),
        check_vma=False,
    )
```

```python
import math

import jax
import jax.numpy as jnp
import numpy as np
from jax import lax
from jax.sharding import PartitionSpec as P

ITERS = 2

AXES = ("wide", "narrow")

highest = lax.Precision.HIGHEST


def cas_matrix(length, columns=None):
    counter = np.arange(length, dtype=np.int64)
    frequency = counter if columns is None else np.asarray(columns, np.int64)
    phase = counter[:, None] * frequency[None, :] % length
    angle = phase.astype(np.float64) * (2.0 * math.pi / length)
    return jnp.asarray((np.cos(angle) + np.sin(angle)).astype(np.float32))


def channel_order(depth, count):
    chunk = depth // count
    if chunk % 2:
        return list(range(depth)), False
    half = chunk // 2
    order = [0, depth // 2]
    for k in range(1, half):
        order += [k, depth - k]
    for k in range(half, depth // 2):
        order += [k, depth - k]
    return order, True


def contract(spec, values, matrix):
    return jnp.einsum(spec, values, matrix, precision=highest, preferred_element_type=jnp.float32)


def exchange(blocks):
    return lax.all_to_all(blocks, AXES, 0, 0, tiled=True)


def global_sums(partials):
    count = lax.axis_size("wide") * lax.axis_size("narrow")
    spread = jnp.broadcast_to(partials[None], (count,) + partials.shape)
    return jnp.sum(exchange(spread), axis=0)


def local(sky_map, noise_weight, power_spectrum):
    local_x, local_y, depth = sky_map.shape
    n_wide = lax.axis_size("wide")
    n_narrow = lax.axis_size("narrow")
    count = n_wide * n_narrow
    chunk = depth // count
    full_x = local_x * n_wide
    full_y = local_y * n_narrow
    matrix_x = cas_matrix(full_x).reshape(n_wide, local_x, full_x)
    matrix_y = cas_matrix(full_y).reshape(n_narrow, local_y, full_y)
    order, paired = channel_order(depth, count)
    matrix_z = cas_matrix(depth, order)
    inverse_cells = 1.0 / float(full_x * full_y * depth)

    def to_planes_of(blocks, rows):
        return blocks.reshape(n_wide, n_narrow, rows, local_x, local_y)

    def to_planes(blocks):
        return blocks.reshape(n_wide, n_narrow, local_x, chunk, local_y)

    def forward_sky(planes):
        along_y = contract("wnakb,nby->kway", planes, matrix_y)
        return contract("kway,wax->xky", along_y, matrix_x)

    def inverse_sky(spectral):
        along_x = contract("xky,wax->kway", spectral, matrix_x)
        along_y = contract("kway,nby->wnakb", along_x, matrix_y)
        return along_y.reshape(count, local_x, chunk, local_y)

    def channel_blocks(values):
        return contract("abz,zdk->dakb", values, matrix_z.reshape(depth, count, chunk))

    def finish(blocks):
        return contract("dakb,zdk->abz", blocks, matrix_z.reshape(depth, count, chunk))

    def smoothed_spectral(blocks, weights):
        return inverse_sky(forward_sky(to_planes(blocks)) * weights)

    right_side = noise_weight * sky_map

    if paired:
        half = chunk // 2
        main = jnp.transpose(power_spectrum[:, :, : depth // 2], (2, 0, 1)).reshape(
            count, half, local_x, local_y
        )
        middle = jnp.broadcast_to(
            power_spectrum[None, None, :, :, depth // 2], (count, 1, local_x, local_y)
        )
        power_blocks = jnp.concatenate([main, middle], axis=1)
        rows = half + 1
    else:
        power_blocks = jnp.transpose(power_spectrum, (2, 0, 1)).reshape(count, chunk, local_x, local_y)
        rows = chunk
    power_received = exchange(power_blocks)
    first = exchange(channel_blocks(noise_weight * right_side))
    power_planes = jnp.transpose(to_planes_of(power_received, rows), (0, 3, 2, 1, 4)).reshape(
        full_x, rows, full_y
    )
    if paired:
        device = lax.axis_index("wide") * n_narrow + lax.axis_index("narrow")
        second = jnp.where(device == 0, power_planes[:, half], power_planes[:, 0])
        weights = jnp.concatenate(
            [power_planes[:, 0:1], second[:, None], jnp.repeat(power_planes[:, 1:half], 2, axis=1)], axis=1
        )
    else:
        weights = power_planes
    weights = weights * inverse_cells

    lanes = 32

    def lane_sums(left, right):
        return jnp.sum(jnp.sum(left * right, axis=(0, 1)).reshape(-1, lanes), axis=0)

    image_1 = right_side + noise_weight * finish(exchange(smoothed_spectral(first, weights)))
    sent = exchange(channel_blocks(noise_weight * image_1))
    returned = smoothed_spectral(sent, weights)
    cross = jnp.sum(sent * returned, axis=(0, 1, 2))
    cross = jnp.pad(cross, (0, lanes - cross.shape[0] % lanes if cross.shape[0] % lanes else 0))
    cross = jnp.sum(cross.reshape(-1, lanes), axis=0)
    image_norm = lane_sums(image_1, image_1)
    partials = jnp.stack(
        [lane_sums(right_side, right_side), lane_sums(right_side, image_1), image_norm, image_norm + cross]
    )
    block = chunk * local_x * local_y
    back = exchange(
        jnp.concatenate(
            [jnp.broadcast_to(partials.reshape(1, 4 * lanes), (count, 4 * lanes)), returned.reshape(count, block)],
            axis=1,
        )
    )
    image_2 = image_1 + noise_weight * finish(back[:, 4 * lanes :].reshape(count, local_x, chunk, local_y))
    summed = jnp.sum(back[:, : 4 * lanes].reshape(count, 4, lanes), axis=0)
    totals = contract("vl,lm->vm", summed, jnp.ones((lanes, depth), jnp.float32))
    moments = totals.reshape(4, 1, 1, depth)
    norm_0, curvature_1, image_norm, cross = moments[0], moments[1], moments[2], moments[3]
    step_1 = norm_0 / curvature_1
    norm_1 = norm_0 - 2.0 * step_1 * curvature_1 + step_1 * step_1 * image_norm
    grow = 1.0 + norm_1 / norm_0
    curvature_2 = grow * grow * curvature_1 - 2.0 * step_1 * grow * image_norm + step_1 * step_1 * cross
    step_2 = norm_1 / curvature_2
    lead = step_1 + step_2 * grow
    tail = step_2 * step_1
    solution = lead * right_side - tail * image_1
    residual = right_side - lead * image_1 + tail * image_2
    return (solution, residual)


def solution(mesh):
    return jax.shard_map(
        local,
        mesh=mesh,
        in_specs=(P("wide", "narrow", None), P("wide", "narrow", None), P("wide", "narrow", None)),
        out_specs=(P("wide", "narrow", None), P("wide", "narrow", None)),
        check_vma=False,
    )
```
